512 devices in a mesh: walk: 32 (over z_lo, y), elec: 16 (over z_hi, x, core).
Axes of the slice: x: 4, y: 4, z: 16 (z_hi: 2, z_lo: 8; z = z_hi * 8 + z_lo), core: 2. Of those that a mesh axis runs over, the one named last changes fastest.
Arguments:
- tokens: bfloat16 [512, 128, 256], P('walk', 'elec'), may hold values from -6 to 6
- positions: float32 [512, 3, 128], P('walk', None, 'elec'), may hold values from -9 to 9
- spin_labels: int32 [128], P('elec'), may hold values from 0 to 1
- system_ids: int32 [512], P('walk'), may hold values from 0 to 7
- filter_weight: bfloat16 [2, 32, 256], replicated, may hold values from -6 to 6
- head_weight: bfloat16 [8, 256, 256], replicated, may hold values from -0.375 to 0.375
- cotangent: bfloat16 [512, 128, 256], P('walk', 'elec'), may hold values from -6 to 6
Outputs:
- layer_out: bfloat16 [512, 128, 256], P('walk', 'elec')
- token_grad: float32 [512, 128, 256], P('walk', 'elec')
- filter_grad: float32 [2, 32, 256], replicated
The draws below stay inside these ranges and needn't reach their ends.
All inputs are finite; a program needn't handle non-finite values.
Results may differ from the reference program's by a relative error of at most 0.012.
Values may be sent and summed in bfloat16 or wider, within the bound.
No kernel may reach another device: no remote copies, remote signals or barrier semaphores. Data moves between devices by JAX's collectives and lax.ppermute only.
A program may use at most 64 MiB of HBM per device.

```python
import math
import jax
import jax.numpy as jnp
from jax import lax

F = 256
K = 32
E_SYS = 8
WALKERS = 512
NEL = 128


def set_ends(values, rng, smallest, largest):
    index_at = [jax.random.randint(jax.random.fold_in(rng, axis), (), 0, length) for axis, length in enumerate(values.shape)]
    longest = values.shape.index(max(values.shape))
    beside = index_at[:longest] + [(index_at[longest] + 1) % values.shape[longest]] + index_at[longest + 1:]
    return values.at[tuple(index_at)].set(smallest).at[tuple(beside)].set(largest)


def block_levels(rng, dims, split, smallest, high):
    def one(dim, parts):
        draws = jax.random.uniform(jax.random.fold_in(jax.random.fold_in(rng, 6), dim), (parts,), jnp.float32, smallest / len(split), high / len(split))
        return jnp.repeat(jnp.exp(draws), dims[dim] // parts).reshape((-1,) + (1,) * (len(dims) - dim - 1))

    factor_of = one(*split[0])
    for cut in split[1:]:
        factor_of = factor_of * one(*cut)
    return factor_of


def centred(rng, extent, spread, reach, shards=(), kind=jnp.bfloat16):
    result = jax.random.normal(rng, extent, jnp.float32) * spread
    if len(shards) > 0:
        result = block_levels(rng, extent, shards, -0.22, 0.18) * result
    return jnp.clip(result, min=-reach, max=reach).astype(kind)


def setup_inputs(seed: int = 0) -> dict:
    key_list = jax.random.split(jax.random.key(seed), 8)
    return {
        "tokens": centred(key_list[0], (WALKERS, NEL, F), 1.0, 6.0, ((0, 32), (1, 16))),
        "positions": centred(key_list[1], (WALKERS, 3, NEL), 1.5, 9.0, ((0, 32), (2, 16)), jnp.float32),
        "spin_labels": set_ends(jax.random.randint(key_list[2], (NEL,), 0, 2), jax.random.fold_in(key_list[2], 1), 0, 1).astype(jnp.int32),
        "system_ids": set_ends(jax.random.randint(key_list[3], (WALKERS,), 0, E_SYS), jax.random.fold_in(key_list[3], 1), 0, E_SYS - 1).astype(jnp.int32),
        "filter_weight": centred(key_list[4], (2, K, F), 1 ** -0.5, 6.0),
        "head_weight": centred(key_list[5], (E_SYS, F, F), F ** -0.5, 0.375),
        "cotangent": centred(key_list[6], (WALKERS, NEL, F), 1.0, 6.0, ((0, 32), (1, 16))),
    }


cutoff_radius = 8.0

def grad_silu(values):
    logistic = jax.nn.sigmoid(values)
    return logistic * (1.0 + values * (1.0 - logistic))

def radial_pairs(walker_pos, spin_labels):
    offsets_xyz = walker_pos[:, :, None] - walker_pos[:, None, :]
    distance = jnp.sqrt(lax.optimization_barrier(jnp.sum(offsets_xyz * offsets_xyz, axis=0)))
    spacing = cutoff_radius / (K - 1)
    centers = jnp.arange(K, dtype=jnp.float32) * spacing
    radial = jnp.exp(-jnp.square((distance[..., None] - centers) / spacing))
    same_spin = (spin_labels[:, None] == spin_labels[None, :])[..., None]
    nothing = jnp.zeros_like(radial)
    both = jnp.concatenate([jnp.where(same_spin, radial, nothing), jnp.where(same_spin, nothing, radial)], axis=-1)
    return both.astype(jnp.bfloat16)

def reference(tokens, positions, spin_labels, system_ids, filter_weight, head_weight, cotangent):
    msg_scale = 1.0 / math.sqrt(NEL)
    grad_scale = 1.0 / math.sqrt(WALKERS * NEL)
    filter_pairs = filter_weight.reshape(2 * K, F)
    rows_idx = jnp.arange(NEL, dtype=jnp.int32)
    off_diag = (rows_idx[:, None] != rows_idx[None, :])[..., None]

    def one_walker(inputs):
        walker_pos, walker_tok, walker_cot, system = inputs
        head_mat = head_weight[system]
        pair_feats = radial_pairs(walker_pos, spin_labels)
        pre_act = jnp.dot(pair_feats.reshape(NEL * NEL, 2 * K), filter_pairs, preferred_element_type=jnp.float32).reshape(NEL, NEL, F)
        filters = jnp.where(off_diag, jax.nn.silu(pre_act), 0.0).astype(jnp.bfloat16)
        messages = (msg_scale * jnp.einsum('ijf,jf->if', filters.astype(jnp.float32), walker_tok.astype(jnp.float32))).astype(jnp.bfloat16)
        head_out = jnp.dot(messages, head_mat, preferred_element_type=jnp.float32)
        layer_out = (walker_tok.astype(jnp.float32) + head_out).astype(jnp.bfloat16)
        msg_grads = jnp.dot(walker_cot, head_mat.T, preferred_element_type=jnp.float32).astype(jnp.bfloat16)
        pre_grad = msg_scale * msg_grads.astype(jnp.float32)[:, None, :] * walker_tok.astype(jnp.float32)[None, :, :] * grad_silu(pre_act)
        pre_grad = jnp.where(off_diag, pre_grad, 0.0).astype(jnp.bfloat16)
        weight_part = jnp.dot(pair_feats.reshape(NEL * NEL, 2 * K).T, pre_grad.reshape(NEL * NEL, F), preferred_element_type=jnp.float32)
        token_grad = walker_cot.astype(jnp.float32) + msg_scale * jnp.einsum('ijf,if->jf', filters.astype(jnp.float32), msg_grads.astype(jnp.float32))
        return (layer_out, token_grad, weight_part)
    layer_out, token_grad, weight_parts = lax.map(one_walker, (positions, tokens, cotangent, system_ids))
    filter_grad = (grad_scale * lax.optimization_barrier(jnp.sum(weight_parts, axis=0))).reshape(2, K, F)
    return (layer_out, token_grad, filter_grad)
```

```python
import math

import jax
import jax.numpy as jnp
from jax import lax
from jax.sharding import PartitionSpec as P

cutoff_radius = 8.0


def grad_silu(values):
    logistic = jax.nn.sigmoid(values)
    return logistic * (1.0 + values * (1.0 - logistic))


def butterfly_sum(values, axes):
    for axis in axes:
        size = lax.axis_size(axis)
        step = 1
        while step < size:
            pairs = [(i, i ^ step) for i in range(size)]
            values = values + lax.ppermute(values, axis, pairs)
            step *= 2
    return values


def body(tokens, positions, spin_labels, system_ids, filter_weight, head_weight, cotangent):
    walkers_dev, elec_dev, features = tokens.shape
    basis_count = filter_weight.shape[1]
    elec_size = lax.axis_size("elec")
    elec_total = elec_dev * elec_size
    walker_total = walkers_dev * lax.axis_size("walk")
    msg_scale = 1.0 / math.sqrt(elec_total)
    grad_scale = 1.0 / math.sqrt(walker_total * elec_total)
    filter_pairs = filter_weight.reshape(2 * basis_count, features)

    spin_f = jnp.broadcast_to(spin_labels.astype(jnp.float32)[None, :, None], (walkers_dev, elec_dev, 1))
    packed = jnp.concatenate(
        [
            tokens.astype(jnp.float32),
            cotangent.astype(jnp.float32),
            jnp.transpose(positions, (0, 2, 1)),
            spin_f,
        ],
        axis=-1,
    )
    whole = lax.all_to_all(packed, "elec", 0, 1, tiled=True)[0]
    walker_tok = whole[:, :features].astype(jnp.bfloat16)
    walker_cot = whole[:, features : 2 * features].astype(jnp.bfloat16)
    walker_pos = whole[:, 2 * features : 2 * features + 3]
    spins = whole[:, 2 * features + 3]

    per_walker = walkers_dev // elec_size
    system = system_ids[lax.axis_index("elec") * per_walker]
    head_mat = lax.dynamic_index_in_dim(head_weight, system, 0, keepdims=False)

    msg_grads = jnp.dot(walker_cot, head_mat.T, preferred_element_type=jnp.float32).astype(jnp.bfloat16)
    tok_f = walker_tok.astype(jnp.float32)
    grads_f = msg_grads.astype(jnp.float32)

    spacing = cutoff_radius / (basis_count - 1)
    centers = jnp.arange(basis_count, dtype=jnp.float32) * spacing
    all_index = jnp.arange(elec_total, dtype=jnp.int32)
    block_rows = math.gcd(elec_total, 32)

    def one_block(block_index, running):
        msg_out, back_out, weight_run = running
        first = block_index * block_rows
        near_pos = lax.dynamic_slice_in_dim(walker_pos, first, block_rows, 0)
        near_spin = lax.dynamic_slice_in_dim(spins, first, block_rows, 0)
        near_grads = lax.dynamic_slice_in_dim(grads_f, first, block_rows, 0)
        near_index = first + jnp.arange(block_rows, dtype=jnp.int32)
        offsets = near_pos[:, None, :] - walker_pos[None, :, :]
        squares = offsets * offsets
        distance = jnp.sqrt(squares[..., 0] + squares[..., 1] + squares[..., 2])
        radial = jnp.exp(-jnp.square((distance[..., None] - centers) / spacing))
        same_spin = (near_spin[:, None] == spins[None, :])[..., None]
        nothing = jnp.zeros_like(radial)
        pair_feats = jnp.concatenate(
            [jnp.where(same_spin, radial, nothing), jnp.where(same_spin, nothing, radial)], axis=-1
        ).astype(jnp.bfloat16)
        pre_act = jnp.einsum("ijk,kf->ijf", pair_feats, filter_pairs, preferred_element_type=jnp.float32)
        off_diag = (near_index[:, None] != all_index[None, :])[..., None]
        filters = jnp.where(off_diag, jax.nn.silu(pre_act), 0.0).astype(jnp.bfloat16).astype(jnp.float32)
        msg_rows = jnp.sum(filters * tok_f[None, :, :], axis=1)
        back_rows = jnp.sum(filters * grads_f[None, :, :], axis=1)
        pre_grad = msg_scale * near_grads[:, None, :] * tok_f[None, :, :] * grad_silu(pre_act)
        pre_grad = jnp.where(off_diag, pre_grad, 0.0).astype(jnp.bfloat16)
        weight_run = weight_run + jnp.einsum(
            "ijk,ijf->kf", pair_feats, pre_grad, preferred_element_type=jnp.float32
        )
        msg_out = lax.dynamic_update_slice_in_dim(msg_out, msg_rows, first, 0)
        back_out = lax.dynamic_update_slice_in_dim(back_out, back_rows, first, 0)
        return (msg_out, back_out, weight_run)

    zero_rows = jnp.zeros((elec_total, features), jnp.float32)
    weight_zero = jnp.zeros((2 * basis_count, features), jnp.float32)
    msg_sum, back_sum, weight_sum = lax.fori_loop(
        0, elec_total // block_rows, one_block, (zero_rows, zero_rows, weight_zero)
    )

    messages = (msg_scale * msg_sum).astype(jnp.bfloat16)
    head_out = jnp.dot(messages, head_mat, preferred_element_type=jnp.float32)
    layer_out = (tok_f + head_out).astype(jnp.bfloat16)
    token_grad = walker_cot.astype(jnp.float32) + msg_scale * back_sum

    weight_total = butterfly_sum(weight_sum, ("elec", "walk"))
    filter_grad = (grad_scale * weight_total).reshape(2, basis_count, features)

    result = jnp.concatenate([layer_out.astype(jnp.float32), token_grad], axis=-1)[None]
    result = lax.all_to_all(result, "elec", 1, 0, tiled=True)
    return (result[..., :features].astype(jnp.bfloat16), result[..., features:], filter_grad)


def solution(mesh):
    in_specs = (
        P("walk", "elec", None),
        P("walk", None, "elec"),
        P("elec"),
        P("walk"),
        P(),
        P(),
        P("walk", "elec", None),
    )
    out_specs = (P("walk", "elec", None), P("walk", "elec", None), P())
    return jax.shard_map(body, mesh=mesh, in_specs=in_specs, out_specs=out_specs, check_vma=False)
```

```python
import math

import jax
import jax.numpy as jnp
from jax import lax
from jax.sharding import PartitionSpec as P

cutoff_radius = 8.0


def grad_silu(values):
    logistic = jax.nn.sigmoid(values)
    return logistic * (1.0 + values * (1.0 - logistic))


def butterfly_sum(values, axes):
    for axis in axes:
        size = lax.axis_size(axis)
        step = 1
        while step < size:
            pairs = [(i, i ^ step) for i in range(size)]
            values = values + lax.ppermute(values, axis, pairs)
            step *= 2
    return values


def body(tokens, positions, spin_labels, system_ids, filter_weight, head_weight, cotangent):
    walkers_dev, elec_dev, features = tokens.shape
    basis_count = filter_weight.shape[1]
    elec_size = lax.axis_size("elec")
    elec_total = elec_dev * elec_size
    walker_total = walkers_dev * lax.axis_size("walk")
    msg_scale = 1.0 / math.sqrt(elec_total)
    grad_scale = 1.0 / math.sqrt(walker_total * elec_total)
    filter_pairs = filter_weight.reshape(2 * basis_count, features)

    pos_t = jnp.transpose(positions, (0, 2, 1))
    hi = lax.reduce_precision(pos_t, exponent_bits=8, mantissa_bits=7)
    rest = pos_t - hi
    mid = lax.reduce_precision(rest, exponent_bits=8, mantissa_bits=7)
    pos_hi = hi.astype(jnp.bfloat16)
    pos_mid = mid.astype(jnp.bfloat16)
    pos_lo = (rest - mid).astype(jnp.bfloat16)
    spin_b = jnp.broadcast_to(spin_labels.astype(jnp.bfloat16)[None, :, None], (walkers_dev, elec_dev, 1))
    packed = jnp.concatenate([tokens, cotangent, pos_hi, pos_mid, pos_lo, spin_b], axis=-1)
    whole = lax.all_to_all(packed, "elec", 0, 1, tiled=True)[0]
    walker_tok = whole[:, :features]
    walker_cot = whole[:, features : 2 * features]
    tail = whole[:, 2 * features :].astype(jnp.float32)
    walker_pos = (tail[:, 0:3] + tail[:, 3:6]) + tail[:, 6:9]
    spins = tail[:, 9]

    per_walker = walkers_dev // elec_size
    system = system_ids[lax.axis_index("elec") * per_walker]
    head_mat = lax.dynamic_index_in_dim(head_weight, system, 0, keepdims=False)

    msg_grads = jnp.dot(walker_cot, head_mat.T, preferred_element_type=jnp.float32).astype(jnp.bfloat16)
    tok_f = walker_tok.astype(jnp.float32)
    grads_f = msg_grads.astype(jnp.float32)

    spacing = cutoff_radius / (basis_count - 1)
    centers = jnp.arange(basis_count, dtype=jnp.float32) * spacing
    all_index = jnp.arange(elec_total, dtype=jnp.int32)
    block_rows = math.gcd(elec_total, 32)

    def one_block(block_index, running):
        msg_out, back_out, weight_run = running
        first = block_index * block_rows
        near_pos = lax.dynamic_slice_in_dim(walker_pos, first, block_rows, 0)
        near_spin = lax.dynamic_slice_in_dim(spins, first, block_rows, 0)
        near_grads = lax.dynamic_slice_in_dim(grads_f, first, block_rows, 0)
        near_index = first + jnp.arange(block_rows, dtype=jnp.int32)
        offsets = near_pos[:, None, :] - walker_pos[None, :, :]
        squares = offsets * offsets
        distance = jnp.sqrt(squares[..., 0] + squares[..., 1] + squares[..., 2])
        radial = jnp.exp(-jnp.square((distance[..., None] - centers) / spacing))
        same_spin = (near_spin[:, None] == spins[None, :])[..., None]
        nothing = jnp.zeros_like(radial)
        pair_feats = jnp.concatenate(
            [jnp.where(same_spin, radial, nothing), jnp.where(same_spin, nothing, radial)], axis=-1
        ).astype(jnp.bfloat16)
        pre_act = jnp.einsum("ijk,kf->ijf", pair_feats, filter_pairs, preferred_element_type=jnp.float32)
        off_diag = (near_index[:, None] != all_index[None, :])[..., None]
        filters = jnp.where(off_diag, jax.nn.silu(pre_act), 0.0).astype(jnp.bfloat16).astype(jnp.float32)
        msg_rows = jnp.sum(filters * tok_f[None, :, :], axis=1)
        back_rows = jnp.sum(filters * grads_f[None, :, :], axis=1)
        pre_grad = msg_scale * near_grads[:, None, :] * tok_f[None, :, :] * grad_silu(pre_act)
        pre_grad = jnp.where(off_diag, pre_grad, 0.0).astype(jnp.bfloat16)
        weight_run = weight_run + jnp.einsum(
            "ijk,ijf->kf", pair_feats, pre_grad, preferred_element_type=jnp.float32
        )
        msg_out = lax.dynamic_update_slice_in_dim(msg_out, msg_rows, first, 0)
        back_out = lax.dynamic_update_slice_in_dim(back_out, back_rows, first, 0)
        return (msg_out, back_out, weight_run)

    zero_rows = jnp.zeros((elec_total, features), jnp.float32)
    weight_zero = jnp.zeros((2 * basis_count, features), jnp.float32)
    msg_sum, back_sum, weight_sum = lax.fori_loop(
        0, elec_total // block_rows, one_block, (zero_rows, zero_rows, weight_zero)
    )

    messages = (msg_scale * msg_sum).astype(jnp.bfloat16)
    head_out = jnp.dot(messages, head_mat, preferred_element_type=jnp.float32)
    layer_out = (tok_f + head_out).astype(jnp.bfloat16)
    token_grad = walker_cot.astype(jnp.float32) + msg_scale * back_sum

    weight_total = butterfly_sum(weight_sum, ("elec", "walk"))
    filter_grad = (grad_scale * weight_total).reshape(2, basis_count, features)

    result = jnp.concatenate([layer_out.astype(jnp.float32), token_grad], axis=-1)[None]
    result = lax.all_to_all(result, "elec", 1, 0, tiled=True)
    return (result[..., :features].astype(jnp.bfloat16), result[..., features:], filter_grad)


def solution(mesh):
    in_specs = (
        P("walk", "elec", None),
        P("walk", None, "elec"),
        P("elec"),
        P("walk"),
        P(),
        P(),
        P("walk", "elec", None),
    )
    out_specs = (P("walk", "elec", None), P("walk", "elec", None), P())
    return jax.shard_map(body, mesh=mesh, in_specs=in_specs, out_specs=out_specs, check_vma=False)
```

```python
import functools
import math

import jax
import jax.numpy as jnp
from jax import lax
from jax.experimental import pallas as pl
from jax.experimental.pallas import tpu as pltpu
from jax.sharding import PartitionSpec as P

cutoff_radius = 8.0


def grad_silu(values):
    logistic = jax.nn.sigmoid(values)
    return logistic * (1.0 + values * (1.0 - logistic))


def butterfly_sum(values, axes):
    for axis in axes:
        size = lax.axis_size(axis)
        step = 1
        while step < size:
            pairs = [(i, i ^ step) for i in range(size)]
            values = values + lax.ppermute(values, axis, pairs)
            step *= 2
    return values


def pair_kernel(pf_ref, pft_ref, w_ref, tok_ref, mg_ref, msg_ref, back_ref, wacc_ref, pg_ref, *, rows, n, scale):
    b = pl.program_id(0)
    @pl.when(b == 0)
    def _():
        wacc_ref[...] = jnp.zeros_like(wacc_ref)
    w = w_ref[...]
    tok = tok_ref[...]
    mg = mg_ref[...]
    col = lax.broadcasted_iota(jnp.int32, (n, 1), 0)
    def row(r, carry):
        i = b * rows + r
        start = pl.multiple_of(r * n, n)
        pre = jnp.dot(pf_ref[pl.ds(start, n), :], w, preferred_element_type=jnp.float32)
        g = 1.0 / (1.0 + jnp.exp(-pre))
        keep = col != i
        filt = jnp.where(keep, pre * g, 0.0).astype(jnp.bfloat16).astype(jnp.float32)
        msg_ref[pl.ds(r, 1), :] = jnp.sum(filt * tok, axis=0, keepdims=True)
        back_ref[pl.ds(r, 1), :] = jnp.sum(filt * mg, axis=0, keepdims=True)
        near = scale * mg_ref[pl.ds(i, 1), :]
        gs = g * (1.0 + pre * (1.0 - g))
        pg = jnp.where(keep, near * tok * gs, 0.0)
        pg_ref[pl.ds(start, n), :] = pg.astype(jnp.bfloat16)
        return carry
    lax.fori_loop(0, rows, row, 0)
    wacc_ref[...] += jnp.dot(pft_ref[...], pg_ref[...], preferred_element_type=jnp.float32)

def pair_block(pf, pft, w, tok, mg, scale, rows=16):
    nn, k2 = pf.shape
    n, f = tok.shape
    kern = functools.partial(pair_kernel, rows=rows, n=n, scale=scale)
    return pl.pallas_call(
        kern,
        grid=(n // rows,),
        in_specs=[
            pl.BlockSpec((rows * n, k2), lambda b: (b, 0)),
            pl.BlockSpec((k2, rows * n), lambda b: (0, b)),
            pl.BlockSpec((k2, f), lambda b: (0, 0)),
            pl.BlockSpec((n, f), lambda b: (0, 0)),
            pl.BlockSpec((n, f), lambda b: (0, 0)),
        ],
        out_specs=[
            pl.BlockSpec((rows, f), lambda b: (b, 0)),
            pl.BlockSpec((rows, f), lambda b: (b, 0)),
            pl.BlockSpec((k2, f), lambda b: (0, 0)),
        ],
        out_shape=[
            jax.ShapeDtypeStruct((n, f), jnp.float32),
            jax.ShapeDtypeStruct((n, f), jnp.float32),
            jax.ShapeDtypeStruct((k2, f), jnp.float32),
        ],
        scratch_shapes=[pltpu.VMEM((rows * n, f), jnp.bfloat16)],
        compiler_params=pltpu.CompilerParams(dimension_semantics=("arbitrary",)),
    )(pf, pft, w, tok, mg)


def body(tokens, positions, spin_labels, system_ids, filter_weight, head_weight, cotangent):
    walkers_dev, elec_dev, features = tokens.shape
    basis_count = filter_weight.shape[1]
    elec_size = lax.axis_size("elec")
    elec_total = elec_dev * elec_size
    walker_total = walkers_dev * lax.axis_size("walk")
    msg_scale = 1.0 / math.sqrt(elec_total)
    grad_scale = 1.0 / math.sqrt(walker_total * elec_total)
    filter_pairs = filter_weight.reshape(2 * basis_count, features)

    pos_t = jnp.transpose(positions, (0, 2, 1))
    hi = lax.reduce_precision(pos_t, exponent_bits=8, mantissa_bits=7)
    rest = pos_t - hi
    mid = lax.reduce_precision(rest, exponent_bits=8, mantissa_bits=7)
    pos_hi = hi.astype(jnp.bfloat16)
    pos_mid = mid.astype(jnp.bfloat16)
    pos_lo = (rest - mid).astype(jnp.bfloat16)
    spin_b = jnp.broadcast_to(spin_labels.astype(jnp.bfloat16)[None, :, None], (walkers_dev, elec_dev, 1))
    packed = jnp.concatenate([tokens, cotangent, pos_hi, pos_mid, pos_lo, spin_b], axis=-1)
    whole = lax.all_to_all(packed, "elec", 0, 1, tiled=True)[0]
    walker_tok = whole[:, :features]
    walker_cot = whole[:, features : 2 * features]
    tail = whole[:, 2 * features :].astype(jnp.float32)
    walker_pos = (tail[:, 0:3] + tail[:, 3:6]) + tail[:, 6:9]
    spins = tail[:, 9]

    per_walker = walkers_dev // elec_size
    system = system_ids[lax.axis_index("elec") * per_walker]
    head_mat = lax.dynamic_index_in_dim(head_weight, system, 0, keepdims=False)

    msg_grads = jnp.dot(walker_cot, head_mat.T, preferred_element_type=jnp.float32).astype(jnp.bfloat16)
    tok_f = walker_tok.astype(jnp.float32)
    grads_f = msg_grads.astype(jnp.float32)

    spacing = cutoff_radius / (basis_count - 1)
    centers = jnp.arange(basis_count, dtype=jnp.float32) * spacing
    offsets = walker_pos[:, None, :] - walker_pos[None, :, :]
    squares = offsets * offsets
    distance = jnp.sqrt(squares[..., 0] + squares[..., 1] + squares[..., 2])
    radial = jnp.exp(-jnp.square((distance[..., None] - centers) / spacing))
    same_spin = (spins[:, None] == spins[None, :])[..., None]
    nothing = jnp.zeros_like(radial)
    pair_feats = jnp.concatenate(
        [jnp.where(same_spin, radial, nothing), jnp.where(same_spin, nothing, radial)], axis=-1
    ).astype(jnp.bfloat16)
    pair_flat = pair_feats.reshape(elec_total * elec_total, 2 * basis_count)
    msg_sum, back_sum, weight_sum = pair_block(
        pair_flat, pair_flat.T, filter_pairs, tok_f, grads_f, msg_scale, rows=math.gcd(elec_total, 16)
    )

    messages = (msg_scale * msg_sum).astype(jnp.bfloat16)
    head_out = jnp.dot(messages, head_mat, preferred_element_type=jnp.float32)
    layer_out = (tok_f + head_out).astype(jnp.bfloat16)
    token_grad = walker_cot.astype(jnp.float32) + msg_scale * back_sum

    weight_total = butterfly_sum(weight_sum, ("elec", "walk"))
    filter_grad = (grad_scale * weight_total).reshape(2, basis_count, features)

    result = jnp.concatenate([layer_out.astype(jnp.float32), token_grad], axis=-1)[None]
    result = lax.all_to_all(result, "elec", 1, 0, tiled=True)
    return (result[..., :features].astype(jnp.bfloat16), result[..., features:], filter_grad)


def solution(mesh):
    in_specs = (
        P("walk", "elec", None),
        P("walk", None, "elec"),
        P("elec"),
        P("walk"),
        P(),
        P(),
        P("walk", "elec", None),
    )
    out_specs = (P("walk", "elec", None), P("walk", "elec", None), P())
    return jax.shard_map(body, mesh=mesh, in_specs=in_specs, out_specs=out_specs, check_vma=False)
```

```python
import math

import jax
import jax.numpy as jnp
from jax import lax
from jax.sharding import PartitionSpec as P

cutoff_radius = 8.0


def grad_silu(values):
    logistic = jax.nn.sigmoid(values)
    return logistic * (1.0 + values * (1.0 - logistic))


def butterfly_sum(values, axes):
    for axis in axes:
        size = lax.axis_size(axis)
        step = 1
        while step < size:
            pairs = [(i, i ^ step) for i in range(size)]
            values = values + lax.ppermute(values, axis, pairs)
            step *= 2
    return values


def body(tokens, positions, spin_labels, system_ids, filter_weight, head_weight, cotangent):
    walkers_dev, elec_dev, features = tokens.shape
    basis_count = filter_weight.shape[1]
    elec_size = lax.axis_size("elec")
    elec_total = elec_dev * elec_size
    walker_total = walkers_dev * lax.axis_size("walk")
    msg_scale = 1.0 / math.sqrt(elec_total)
    grad_scale = 1.0 / math.sqrt(walker_total * elec_total)
    filter_pairs = filter_weight.reshape(2 * basis_count, features)

    pos_t = jnp.transpose(positions, (0, 2, 1))
    hi = lax.reduce_precision(pos_t, exponent_bits=8, mantissa_bits=7)
    rest = pos_t - hi
    mid = lax.reduce_precision(rest, exponent_bits=8, mantissa_bits=7)
    pos_hi = hi.astype(jnp.bfloat16)
    pos_mid = mid.astype(jnp.bfloat16)
    pos_lo = (rest - mid).astype(jnp.bfloat16)
    spin_b = jnp.broadcast_to(spin_labels.astype(jnp.bfloat16)[None, :, None], (walkers_dev, elec_dev, 1))
    packed = jnp.concatenate([tokens, cotangent, pos_hi, pos_mid, pos_lo, spin_b], axis=-1)
    whole = lax.all_to_all(packed, "elec", 0, 1, tiled=True)[0]
    walker_tok = whole[:, :features]
    walker_cot = whole[:, features : 2 * features]
    tail = whole[:, 2 * features :].astype(jnp.float32)
    walker_pos = (tail[:, 0:3] + tail[:, 3:6]) + tail[:, 6:9]
    spins = tail[:, 9]

    per_walker = walkers_dev // elec_size
    system = system_ids[lax.axis_index("elec") * per_walker]
    head_mat = lax.dynamic_index_in_dim(head_weight, system, 0, keepdims=False)

    msg_grads = jnp.dot(walker_cot, head_mat.T, preferred_element_type=jnp.float32).astype(jnp.bfloat16)
    tok_f = walker_tok.astype(jnp.float32)
    grads_f = msg_grads.astype(jnp.float32)

    spacing = cutoff_radius / (basis_count - 1)
    centers = jnp.arange(basis_count, dtype=jnp.float32) * spacing
    all_index = jnp.arange(elec_total, dtype=jnp.int32)
    block_rows = math.gcd(elec_total, 32)

    def one_block(block_index, running):
        msg_out, back_out, weight_run = running
        first = block_index * block_rows
        near_pos = lax.dynamic_slice_in_dim(walker_pos, first, block_rows, 0)
        near_spin = lax.dynamic_slice_in_dim(spins, first, block_rows, 0)
        near_grads = lax.dynamic_slice_in_dim(grads_f, first, block_rows, 0)
        near_index = first + jnp.arange(block_rows, dtype=jnp.int32)
        offsets = near_pos[:, None, :] - walker_pos[None, :, :]
        squares = offsets * offsets
        distance = jnp.sqrt(squares[..., 0] + squares[..., 1] + squares[..., 2])
        radial = jnp.exp(-jnp.square((distance[..., None] - centers) / spacing))
        same_spin = (near_spin[:, None] == spins[None, :])[..., None]
        nothing = jnp.zeros_like(radial)
        pair_feats = jnp.concatenate(
            [jnp.where(same_spin, radial, nothing), jnp.where(same_spin, nothing, radial)], axis=-1
        ).astype(jnp.bfloat16)
        pre_act = jnp.einsum("ijk,kf->ijf", pair_feats, filter_pairs, preferred_element_type=jnp.float32)
        off_diag = (near_index[:, None] != all_index[None, :])[..., None]
        filters = jnp.where(off_diag, jax.nn.silu(pre_act), 0.0).astype(jnp.bfloat16).astype(jnp.float32)
        msg_rows = jnp.sum(filters * tok_f[None, :, :], axis=1)
        back_rows = jnp.sum(filters * grads_f[None, :, :], axis=1)
        pre_grad = msg_scale * near_grads[:, None, :] * tok_f[None, :, :] * grad_silu(pre_act)
        pre_grad = jnp.where(off_diag, pre_grad, 0.0).astype(jnp.bfloat16)
        weight_run = weight_run + jnp.einsum(
            "ijk,ijf->kf", pair_feats, pre_grad, preferred_element_type=jnp.float32
        )
        msg_out = lax.dynamic_update_slice_in_dim(msg_out, msg_rows, first, 0)
        back_out = lax.dynamic_update_slice_in_dim(back_out, back_rows, first, 0)
        return (msg_out, back_out, weight_run)

    zero_rows = jnp.zeros((elec_total, features), jnp.float32)
    weight_zero = jnp.zeros((2 * basis_count, features), jnp.float32)
    msg_sum, back_sum, weight_sum = lax.fori_loop(
        0, elec_total // block_rows, one_block, (zero_rows, zero_rows, weight_zero)
    )

    messages = (msg_scale * msg_sum).astype(jnp.bfloat16)
    head_out = jnp.dot(messages, head_mat, preferred_element_type=jnp.float32)
    layer_out = (tok_f + head_out).astype(jnp.bfloat16)
    token_grad = walker_cot.astype(jnp.float32) + msg_scale * back_sum

    weight_total = butterfly_sum(weight_sum, ("walk", "elec"))
    filter_grad = (grad_scale * weight_total).reshape(2, basis_count, features)

    result = jnp.concatenate([layer_out.astype(jnp.float32), token_grad], axis=-1)[None]
    result = lax.all_to_all(result, "elec", 1, 0, tiled=True)
    return (result[..., :features].astype(jnp.bfloat16), result[..., features:], filter_grad)


def solution(mesh):
    in_specs = (
        P("walk", "elec", None),
        P("walk", None, "elec"),
        P("elec"),
        P("walk"),
        P(),
        P(),
        P("walk", "elec", None),
    )
    out_specs = (P("walk", "elec", None), P("walk", "elec", None), P())
    return jax.shard_map(body, mesh=mesh, in_specs=in_specs, out_specs=out_specs, check_vma=False)
```

```python
import math

import jax
import jax.numpy as jnp
from jax import lax
from jax.sharding import PartitionSpec as P

cutoff_radius = 8.0


def grad_silu(values):
    logistic = jax.nn.sigmoid(values)
    return logistic * (1.0 + values * (1.0 - logistic))


def butterfly_sum(values, axes):
    for axis in axes:
        size = lax.axis_size(axis)
        step = 1
        while step < size:
            pairs = [(i, i ^ step) for i in range(size)]
            values = values + lax.ppermute(values, axis, pairs)
            step *= 2
    return values


def body(tokens, positions, spin_labels, system_ids, filter_weight, head_weight, cotangent):
    walkers_dev, elec_dev, features = tokens.shape
    basis_count = filter_weight.shape[1]
    elec_size = lax.axis_size("elec")
    elec_total = elec_dev * elec_size
    walker_total = walkers_dev * lax.axis_size("walk")
    msg_scale = 1.0 / math.sqrt(elec_total)
    grad_scale = 1.0 / math.sqrt(walker_total * elec_total)
    filter_pairs = filter_weight.reshape(2 * basis_count, features)

    pos_t = jnp.transpose(positions, (0, 2, 1))
    hi = lax.reduce_precision(pos_t, exponent_bits=8, mantissa_bits=7)
    rest = pos_t - hi
    mid = lax.reduce_precision(rest, exponent_bits=8, mantissa_bits=7)
    pos_hi = hi.astype(jnp.bfloat16)
    pos_mid = mid.astype(jnp.bfloat16)
    pos_lo = (rest - mid).astype(jnp.bfloat16)
    spin_b = jnp.broadcast_to(spin_labels.astype(jnp.bfloat16)[None, :, None], (walkers_dev, elec_dev, 1))
    packed = jnp.concatenate([tokens, cotangent, pos_hi, pos_mid, pos_lo, spin_b], axis=-1)
    whole = lax.all_to_all(packed, "elec", 0, 1, tiled=True)[0]
    walker_tok = whole[:, :features]
    walker_cot = whole[:, features : 2 * features]
    tail = whole[:, 2 * features :].astype(jnp.float32)
    walker_pos = (tail[:, 0:3] + tail[:, 3:6]) + tail[:, 6:9]
    spins = tail[:, 9]

    per_walker = walkers_dev // elec_size
    system = system_ids[lax.axis_index("elec") * per_walker]
    head_mat = lax.dynamic_index_in_dim(head_weight, system, 0, keepdims=False)

    msg_grads = jnp.dot(walker_cot, head_mat.T, preferred_element_type=jnp.float32).astype(jnp.bfloat16)
    tok_f = walker_tok.astype(jnp.float32)
    grads_f = msg_grads.astype(jnp.float32)

    spacing = cutoff_radius / (basis_count - 1)
    centers = jnp.arange(basis_count, dtype=jnp.float32) * spacing
    block_rows = math.gcd(elec_total, 32)
    block_count = elec_total // block_rows
    scaled_grads = msg_scale * grads_f

    def pair_terms(first_i, first_j):
        pos_i = walker_pos[first_i : first_i + block_rows]
        pos_j = walker_pos[first_j : first_j + block_rows]
        offsets = pos_i[:, None, :] - pos_j[None, :, :]
        squares = offsets * offsets
        distance = jnp.sqrt(squares[..., 0] + squares[..., 1] + squares[..., 2])
        radial = jnp.exp(-jnp.square((distance[..., None] - centers) / spacing))
        same_spin = (spins[first_i : first_i + block_rows, None] == spins[None, first_j : first_j + block_rows])[..., None]
        nothing = jnp.zeros_like(radial)
        pair_feats = jnp.concatenate(
            [jnp.where(same_spin, radial, nothing), jnp.where(same_spin, nothing, radial)], axis=-1
        ).astype(jnp.bfloat16)
        pre_act = jnp.einsum("ijk,kf->ijf", pair_feats, filter_pairs, preferred_element_type=jnp.float32)
        return pair_feats, pre_act

    msg_parts = [[] for _ in range(block_count)]
    back_parts = [[] for _ in range(block_count)]
    weight_sum = jnp.zeros((2 * basis_count, features), jnp.float32)
    local = jnp.arange(block_rows, dtype=jnp.int32)
    off_diag = (local[:, None] != local[None, :])[..., None]
    for bi in range(block_count):
        fi = bi * block_rows
        tok_i, grads_i, sg_i = (a[fi : fi + block_rows] for a in (tok_f, grads_f, scaled_grads))
        for bj in range(bi, block_count):
            fj = bj * block_rows
            tok_j, grads_j, sg_j = (a[fj : fj + block_rows] for a in (tok_f, grads_f, scaled_grads))
            pair_feats, pre_act = pair_terms(fi, fj)
            if bi == bj:
                filters = jnp.where(off_diag, jax.nn.silu(pre_act), 0.0).astype(jnp.bfloat16).astype(jnp.float32)
                msg_parts[bi].append(jnp.sum(filters * tok_j[None], axis=1))
                back_parts[bi].append(jnp.sum(filters * grads_j[None], axis=1))
                pre_grad = sg_i[:, None, :] * tok_j[None] * grad_silu(pre_act)
                pre_grad = jnp.where(off_diag, pre_grad, 0.0).astype(jnp.bfloat16)
                weight_sum = weight_sum + jnp.einsum(
                    "ijk,ijf->kf", pair_feats, pre_grad, preferred_element_type=jnp.float32
                )
            else:
                filters = jax.nn.silu(pre_act).astype(jnp.bfloat16).astype(jnp.float32)
                msg_parts[bi].append(jnp.sum(filters * tok_j[None], axis=1))
                back_parts[bi].append(jnp.sum(filters * grads_j[None], axis=1))
                msg_parts[bj].append(jnp.sum(filters * tok_i[:, None], axis=0))
                back_parts[bj].append(jnp.sum(filters * grads_i[:, None], axis=0))
                slope = grad_silu(pre_act)
                grad_ij = (sg_i[:, None, :] * tok_j[None] * slope).astype(jnp.bfloat16)
                grad_ji = (sg_j[None, :, :] * tok_i[:, None] * slope).astype(jnp.bfloat16)
                weight_sum = weight_sum + jnp.einsum(
                    "ijk,ijf->kf",
                    jnp.concatenate([pair_feats, pair_feats], axis=1),
                    jnp.concatenate([grad_ij, grad_ji], axis=1),
                    preferred_element_type=jnp.float32,
                )
    msg_sum = jnp.concatenate([sum(p) for p in msg_parts], axis=0)
    back_sum = jnp.concatenate([sum(p) for p in back_parts], axis=0)

    messages = (msg_scale * msg_sum).astype(jnp.bfloat16)
    head_out = jnp.dot(messages, head_mat, preferred_element_type=jnp.float32)
    layer_out = (tok_f + head_out).astype(jnp.bfloat16)
    token_grad = walker_cot.astype(jnp.float32) + msg_scale * back_sum

    weight_total = butterfly_sum(weight_sum, ("walk", "elec"))
    filter_grad = (grad_scale * weight_total).reshape(2, basis_count, features)

    result = jnp.concatenate([layer_out.astype(jnp.float32), token_grad], axis=-1)[None]
    result = lax.all_to_all(result, "elec", 1, 0, tiled=True)
    return (result[..., :features].astype(jnp.bfloat16), result[..., features:], filter_grad)


def solution(mesh):
    in_specs = (
        P("walk", "elec", None),
        P("walk", None, "elec"),
        P("elec"),
        P("walk"),
        P(),
        P(),
        P("walk", "elec", None),
    )
    out_specs = (P("walk", "elec", None), P("walk", "elec", None), P())
    return jax.shard_map(body, mesh=mesh, in_specs=in_specs, out_specs=out_specs, check_vma=False)
```

```python
import math

import jax
import jax.numpy as jnp
from jax import lax
from jax.sharding import PartitionSpec as P

cutoff_radius = 8.0


def grad_silu(values):
    logistic = jax.nn.sigmoid(values)
    return logistic * (1.0 + values * (1.0 - logistic))


def butterfly_sum(values, axes):
    for axis in axes:
        size = lax.axis_size(axis)
        step = 1
        while step < size:
            pairs = [(i, i ^ step) for i in range(size)]
            values = values + lax.ppermute(values, axis, pairs)
            step *= 2
    return values


def body(tokens, positions, spin_labels, system_ids, filter_weight, head_weight, cotangent):
    walkers_dev, elec_dev, features = tokens.shape
    basis_count = filter_weight.shape[1]
    elec_size = lax.axis_size("elec")
    elec_total = elec_dev * elec_size
    walker_total = walkers_dev * lax.axis_size("walk")
    msg_scale = 1.0 / math.sqrt(elec_total)
    grad_scale = 1.0 / math.sqrt(walker_total * elec_total)
    filter_pairs = filter_weight.reshape(2 * basis_count, features)

    pos_t = jnp.transpose(positions, (0, 2, 1))
    hi = lax.reduce_precision(pos_t, exponent_bits=8, mantissa_bits=7)
    rest = pos_t - hi
    mid = lax.reduce_precision(rest, exponent_bits=8, mantissa_bits=7)
    pos_hi = hi.astype(jnp.bfloat16)
    pos_mid = mid.astype(jnp.bfloat16)
    pos_lo = (rest - mid).astype(jnp.bfloat16)
    spin_b = jnp.broadcast_to(spin_labels.astype(jnp.bfloat16)[None, :, None], (walkers_dev, elec_dev, 1))
    packed = jnp.concatenate([tokens, cotangent, pos_hi, pos_mid, pos_lo, spin_b], axis=-1)
    whole = lax.all_to_all(packed, "elec", 0, 1, tiled=True)[0]
    walker_tok = whole[:, :features]
    walker_cot = whole[:, features : 2 * features]
    tail = whole[:, 2 * features :].astype(jnp.float32)
    walker_pos = (tail[:, 0:3] + tail[:, 3:6]) + tail[:, 6:9]
    spins = tail[:, 9]

    per_walker = walkers_dev // elec_size
    system = system_ids[lax.axis_index("elec") * per_walker]
    head_mat = lax.dynamic_index_in_dim(head_weight, system, 0, keepdims=False)

    msg_grads = jnp.dot(walker_cot, head_mat.T, preferred_element_type=jnp.float32).astype(jnp.bfloat16)
    tok_f = walker_tok.astype(jnp.float32)
    grads_f = msg_grads.astype(jnp.float32)

    spacing = cutoff_radius / (basis_count - 1)
    centers = jnp.arange(basis_count, dtype=jnp.float32) * spacing
    all_index = jnp.arange(elec_total, dtype=jnp.int32)
    block_rows = math.gcd(elec_total, 64)
    scaled_grads = msg_scale * grads_f

    def one_block(block_index, running):
        msg_out, back_out, weight_run = running
        first = block_index * block_rows
        near_pos = lax.dynamic_slice_in_dim(walker_pos, first, block_rows, 0)
        near_spin = lax.dynamic_slice_in_dim(spins, first, block_rows, 0)
        near_grads = lax.dynamic_slice_in_dim(scaled_grads, first, block_rows, 0)
        near_index = first + jnp.arange(block_rows, dtype=jnp.int32)
        offsets = near_pos[:, None, :] - walker_pos[None, :, :]
        squares = offsets * offsets
        distance = jnp.sqrt(squares[..., 0] + squares[..., 1] + squares[..., 2])
        radial = jnp.exp(-jnp.square((distance[..., None] - centers) / spacing))
        same_spin = (near_spin[:, None] == spins[None, :])[..., None]
        nothing = jnp.zeros_like(radial)
        pair_feats = jnp.concatenate(
            [jnp.where(same_spin, radial, nothing), jnp.where(same_spin, nothing, radial)], axis=-1
        ).astype(jnp.bfloat16)
        pre_act = jnp.einsum("ijk,kf->ijf", pair_feats, filter_pairs, preferred_element_type=jnp.float32)
        off_diag = (near_index[:, None] != all_index[None, :])[..., None]
        filters = jnp.where(off_diag, jax.nn.silu(pre_act), 0.0).astype(jnp.bfloat16).astype(jnp.float32)
        msg_rows = jnp.sum(filters * tok_f[None, :, :], axis=1)
        back_rows = jnp.sum(filters * grads_f[None, :, :], axis=1)
        pre_grad = near_grads[:, None, :] * tok_f[None, :, :] * grad_silu(pre_act)
        pre_grad = jnp.where(off_diag, pre_grad, 0.0).astype(jnp.bfloat16)
        weight_run = weight_run + jnp.einsum(
            "ijk,ijf->kf", pair_feats, pre_grad, preferred_element_type=jnp.float32
        )
        msg_out = lax.dynamic_update_slice_in_dim(msg_out, msg_rows, first, 0)
        back_out = lax.dynamic_update_slice_in_dim(back_out, back_rows, first, 0)
        return (msg_out, back_out, weight_run)

    zero_rows = jnp.zeros((elec_total, features), jnp.float32)
    weight_zero = jnp.zeros((2 * basis_count, features), jnp.float32)
    msg_sum, back_sum, weight_sum = lax.fori_loop(
        0, elec_total // block_rows, one_block, (zero_rows, zero_rows, weight_zero)
    )

    messages = (msg_scale * msg_sum).astype(jnp.bfloat16)
    head_out = jnp.dot(messages, head_mat, preferred_element_type=jnp.float32)
    layer_out = (tok_f + head_out).astype(jnp.bfloat16)
    token_grad = walker_cot.astype(jnp.float32) + msg_scale * back_sum

    weight_total = butterfly_sum(weight_sum, ("walk", "elec"))
    filter_grad = (grad_scale * weight_total).reshape(2, basis_count, features)

    result = jnp.concatenate([layer_out.astype(jnp.float32), token_grad], axis=-1)[None]
    result = lax.all_to_all(result, "elec", 1, 0, tiled=True)
    return (result[..., :features].astype(jnp.bfloat16), result[..., features:], filter_grad)


def solution(mesh):
    in_specs = (
        P("walk", "elec", None),
        P("walk", None, "elec"),
        P("elec"),
        P("walk"),
        P(),
        P(),
        P("walk", "elec", None),
    )
    out_specs = (P("walk", "elec", None), P("walk", "elec", None), P())
    return jax.shard_map(body, mesh=mesh, in_specs=in_specs, out_specs=out_specs, check_vma=False)
```

```python
import math

import jax
import jax.numpy as jnp
from jax import lax
from jax.sharding import PartitionSpec as P

cutoff_radius = 8.0


def grad_silu(values):
    logistic = jax.nn.sigmoid(values)
    return logistic * (1.0 + values * (1.0 - logistic))


def butterfly_sum(values, axes):
    for axis in axes:
        size = lax.axis_size(axis)
        step = 1
        while step < size:
            pairs = [(i, i ^ step) for i in range(size)]
            values = values + lax.ppermute(values, axis, pairs)
            step *= 2
    return values


def body(tokens, positions, spin_labels, system_ids, filter_weight, head_weight, cotangent):
    walkers_dev, elec_dev, features = tokens.shape
    basis_count = filter_weight.shape[1]
    elec_size = lax.axis_size("elec")
    elec_total = elec_dev * elec_size
    walker_total = walkers_dev * lax.axis_size("walk")
    msg_scale = 1.0 / math.sqrt(elec_total)
    grad_scale = 1.0 / math.sqrt(walker_total * elec_total)
    filter_pairs = filter_weight.reshape(2 * basis_count, features)

    pos_t = jnp.transpose(positions, (0, 2, 1))
    hi = lax.reduce_precision(pos_t, exponent_bits=8, mantissa_bits=7)
    rest = pos_t - hi
    mid = lax.reduce_precision(rest, exponent_bits=8, mantissa_bits=7)
    pos_hi = hi.astype(jnp.bfloat16)
    pos_mid = mid.astype(jnp.bfloat16)
    pos_lo = (rest - mid).astype(jnp.bfloat16)
    spin_b = jnp.broadcast_to(spin_labels.astype(jnp.bfloat16)[None, :, None], (walkers_dev, elec_dev, 1))
    tail_pad = jnp.zeros((walkers_dev, elec_dev, 128 - 10), jnp.bfloat16)
    packed = jnp.concatenate([tokens, cotangent, pos_hi, pos_mid, pos_lo, spin_b, tail_pad], axis=-1)
    whole = lax.all_to_all(packed, "elec", 0, 1, tiled=True)[0]
    walker_tok = whole[:, :features]
    walker_cot = whole[:, features : 2 * features]
    tail = whole[:, 2 * features :].astype(jnp.float32)
    walker_pos = (tail[:, 0:3] + tail[:, 3:6]) + tail[:, 6:9]
    spins = tail[:, 9]

    per_walker = walkers_dev // elec_size
    system = system_ids[lax.axis_index("elec") * per_walker]
    head_mat = lax.dynamic_index_in_dim(head_weight, system, 0, keepdims=False)

    msg_grads = jnp.dot(walker_cot, head_mat.T, preferred_element_type=jnp.float32).astype(jnp.bfloat16)
    tok_f = walker_tok.astype(jnp.float32)
    grads_f = msg_grads.astype(jnp.float32)

    spacing = cutoff_radius / (basis_count - 1)
    centers = jnp.arange(basis_count, dtype=jnp.float32) * spacing
    all_index = jnp.arange(elec_total, dtype=jnp.int32)
    block_rows = math.gcd(elec_total, 64)
    scaled_grads = msg_scale * grads_f

    def one_block(block_index, running):
        msg_out, back_out, weight_run = running
        first = block_index * block_rows
        near_pos = lax.dynamic_slice_in_dim(walker_pos, first, block_rows, 0)
        near_spin = lax.dynamic_slice_in_dim(spins, first, block_rows, 0)
        near_grads = lax.dynamic_slice_in_dim(scaled_grads, first, block_rows, 0)
        near_index = first + jnp.arange(block_rows, dtype=jnp.int32)
        offsets = near_pos[:, None, :] - walker_pos[None, :, :]
        squares = offsets * offsets
        distance = jnp.sqrt(squares[..., 0] + squares[..., 1] + squares[..., 2])
        radial = jnp.exp(-jnp.square((distance[..., None] - centers) / spacing))
        same_spin = (near_spin[:, None] == spins[None, :])[..., None]
        nothing = jnp.zeros_like(radial)
        pair_feats = jnp.concatenate(
            [jnp.where(same_spin, radial, nothing), jnp.where(same_spin, nothing, radial)], axis=-1
        ).astype(jnp.bfloat16)
        pre_act = jnp.einsum("ijk,kf->ijf", pair_feats, filter_pairs, preferred_element_type=jnp.float32)
        off_diag = (near_index[:, None] != all_index[None, :])[..., None]
        filters = jnp.where(off_diag, jax.nn.silu(pre_act), 0.0).astype(jnp.bfloat16).astype(jnp.float32)
        msg_rows = jnp.sum(filters * tok_f[None, :, :], axis=1)
        back_rows = jnp.sum(filters * grads_f[None, :, :], axis=1)
        pre_grad = near_grads[:, None, :] * tok_f[None, :, :] * grad_silu(pre_act)
        pre_grad = jnp.where(off_diag, pre_grad, 0.0).astype(jnp.bfloat16)
        weight_run = weight_run + jnp.einsum(
            "ijk,ijf->kf", pair_feats, pre_grad, preferred_element_type=jnp.float32
        )
        msg_out = lax.dynamic_update_slice_in_dim(msg_out, msg_rows, first, 0)
        back_out = lax.dynamic_update_slice_in_dim(back_out, back_rows, first, 0)
        return (msg_out, back_out, weight_run)

    zero_rows = jnp.zeros((elec_total, features), jnp.float32)
    weight_zero = jnp.zeros((2 * basis_count, features), jnp.float32)
    msg_sum, back_sum, weight_sum = lax.fori_loop(
        0, elec_total // block_rows, one_block, (zero_rows, zero_rows, weight_zero)
    )

    messages = (msg_scale * msg_sum).astype(jnp.bfloat16)
    head_out = jnp.dot(messages, head_mat, preferred_element_type=jnp.float32)
    layer_out = (tok_f + head_out).astype(jnp.bfloat16)
    token_grad = walker_cot.astype(jnp.float32) + msg_scale * back_sum

    weight_total = butterfly_sum(weight_sum, ("walk", "elec"))
    filter_grad = (grad_scale * weight_total).reshape(2, basis_count, features)

    result = jnp.concatenate([layer_out.astype(jnp.float32), token_grad], axis=-1)[None]
    result = lax.all_to_all(result, "elec", 1, 0, tiled=True)
    return (result[..., :features].astype(jnp.bfloat16), result[..., features:], filter_grad)


def solution(mesh):
    in_specs = (
        P("walk", "elec", None),
        P("walk", None, "elec"),
        P("elec"),
        P("walk"),
        P(),
        P(),
        P("walk", "elec", None),
    )
    out_specs = (P("walk", "elec", None), P("walk", "elec", None), P())
    return jax.shard_map(body, mesh=mesh, in_specs=in_specs, out_specs=out_specs, check_vma=False)
```

```python
import math

import jax
import jax.numpy as jnp
from jax import lax
from jax.sharding import PartitionSpec as P

cutoff_radius = 8.0


def logistic(values):
    return 0.5 * jnp.tanh(0.5 * values) + 0.5


def butterfly_sum(values, axes):
    for axis in axes:
        size = lax.axis_size(axis)
        step = 1
        while step < size:
            pairs = [(i, i ^ step) for i in range(size)]
            values = values + lax.ppermute(values, axis, pairs)
            step *= 2
    return values


def body(tokens, positions, spin_labels, system_ids, filter_weight, head_weight, cotangent):
    walkers_dev, elec_dev, features = tokens.shape
    basis_count = filter_weight.shape[1]
    elec_size = lax.axis_size("elec")
    elec_total = elec_dev * elec_size
    walker_total = walkers_dev * lax.axis_size("walk")
    msg_scale = 1.0 / math.sqrt(elec_total)
    grad_scale = 1.0 / math.sqrt(walker_total * elec_total)
    filter_pairs = filter_weight.reshape(2 * basis_count, features)

    pos_t = jnp.transpose(positions, (0, 2, 1))
    hi = lax.reduce_precision(pos_t, exponent_bits=8, mantissa_bits=7)
    rest = pos_t - hi
    mid = lax.reduce_precision(rest, exponent_bits=8, mantissa_bits=7)
    pos_hi = hi.astype(jnp.bfloat16)
    pos_mid = mid.astype(jnp.bfloat16)
    pos_lo = (rest - mid).astype(jnp.bfloat16)
    spin_b = jnp.broadcast_to(spin_labels.astype(jnp.bfloat16)[None, :, None], (walkers_dev, elec_dev, 1))
    packed = jnp.concatenate([tokens, cotangent, pos_hi, pos_mid, pos_lo, spin_b], axis=-1)
    whole = lax.all_to_all(packed, "elec", 0, 1, tiled=True)[0]
    walker_tok = whole[:, :features]
    walker_cot = whole[:, features : 2 * features]
    tail = whole[:, 2 * features :].astype(jnp.float32)
    walker_pos = (tail[:, 0:3] + tail[:, 3:6]) + tail[:, 6:9]
    spins = tail[:, 9]

    per_walker = walkers_dev // elec_size
    system = system_ids[lax.axis_index("elec") * per_walker]
    head_mat = lax.dynamic_index_in_dim(head_weight, system, 0, keepdims=False)

    msg_grads = jnp.dot(walker_cot, head_mat.T, preferred_element_type=jnp.float32).astype(jnp.bfloat16)
    tok_f = walker_tok.astype(jnp.float32)
    grads_f = msg_grads.astype(jnp.float32)

    spacing = cutoff_radius / (basis_count - 1)
    centers = jnp.arange(basis_count, dtype=jnp.float32) * spacing
    all_index = jnp.arange(elec_total, dtype=jnp.int32)
    block_rows = math.gcd(elec_total, 64)
    scaled_grads = msg_scale * grads_f

    def one_block(block_index, running):
        msg_out, back_out, weight_run = running
        first = block_index * block_rows
        near_pos = lax.dynamic_slice_in_dim(walker_pos, first, block_rows, 0)
        near_spin = lax.dynamic_slice_in_dim(spins, first, block_rows, 0)
        near_grads = lax.dynamic_slice_in_dim(scaled_grads, first, block_rows, 0)
        near_index = first + jnp.arange(block_rows, dtype=jnp.int32)
        offsets = near_pos[:, None, :] - walker_pos[None, :, :]
        squares = offsets * offsets
        distance = jnp.sqrt(squares[..., 0] + squares[..., 1] + squares[..., 2])
        radial = jnp.exp(-jnp.square((distance[..., None] - centers) / spacing))
        same_spin = (near_spin[:, None] == spins[None, :])[..., None]
        nothing = jnp.zeros_like(radial)
        pair_feats = jnp.concatenate(
            [jnp.where(same_spin, radial, nothing), jnp.where(same_spin, nothing, radial)], axis=-1
        ).astype(jnp.bfloat16)
        pre_act = jnp.einsum("ijk,kf->ijf", pair_feats, filter_pairs, preferred_element_type=jnp.float32)
        off_diag = (near_index[:, None] != all_index[None, :])[..., None]
        gate = logistic(pre_act)
        filters = jnp.where(off_diag, pre_act * gate, 0.0).astype(jnp.bfloat16).astype(jnp.float32)
        msg_rows = jnp.sum(filters * tok_f[None, :, :], axis=1)
        back_rows = jnp.sum(filters * grads_f[None, :, :], axis=1)
        slope = gate * (1.0 + pre_act * (1.0 - gate))
        pre_grad = near_grads[:, None, :] * tok_f[None, :, :] * slope
        pre_grad = jnp.where(off_diag, pre_grad, 0.0).astype(jnp.bfloat16)
        weight_run = weight_run + jnp.einsum(
            "ijk,ijf->kf", pair_feats, pre_grad, preferred_element_type=jnp.float32
        )
        msg_out = lax.dynamic_update_slice_in_dim(msg_out, msg_rows, first, 0)
        back_out = lax.dynamic_update_slice_in_dim(back_out, back_rows, first, 0)
        return (msg_out, back_out, weight_run)

    zero_rows = jnp.zeros((elec_total, features), jnp.float32)
    weight_zero = jnp.zeros((2 * basis_count, features), jnp.float32)
    msg_sum, back_sum, weight_sum = lax.fori_loop(
        0, elec_total // block_rows, one_block, (zero_rows, zero_rows, weight_zero)
    )

    messages = (msg_scale * msg_sum).astype(jnp.bfloat16)
    head_out = jnp.dot(messages, head_mat, preferred_element_type=jnp.float32)
    layer_out = (tok_f + head_out).astype(jnp.bfloat16)
    token_grad = walker_cot.astype(jnp.float32) + msg_scale * back_sum

    weight_total = butterfly_sum(weight_sum, ("walk", "elec"))
    filter_grad = (grad_scale * weight_total).reshape(2, basis_count, features)

    result = jnp.concatenate([layer_out.astype(jnp.float32), token_grad], axis=-1)[None]
    result = lax.all_to_all(result, "elec", 1, 0, tiled=True)
    return (result[..., :features].astype(jnp.bfloat16), result[..., features:], filter_grad)


def solution(mesh):
    in_specs = (
        P("walk", "elec", None),
        P("walk", None, "elec"),
        P("elec"),
        P("walk"),
        P(),
        P(),
        P("walk", "elec", None),
    )
    out_specs = (P("walk", "elec", None), P("walk", "elec", None), P())
    return jax.shard_map(body, mesh=mesh, in_specs=in_specs, out_specs=out_specs, check_vma=False)
```

```python
import math

import jax
import jax.numpy as jnp
from jax import lax
from jax.sharding import PartitionSpec as P

cutoff_radius = 8.0


def logistic(values):
    return 0.5 * jnp.tanh(0.5 * values) + 0.5


def butterfly_sum(values, axes):
    for axis in axes:
        size = lax.axis_size(axis)
        step = 1
        while step < size:
            pairs = [(i, i ^ step) for i in range(size)]
            values = values + lax.ppermute(values, axis, pairs)
            step *= 2
    return values


def body(tokens, positions, spin_labels, system_ids, filter_weight, head_weight, cotangent):
    walkers_dev, elec_dev, features = tokens.shape
    basis_count = filter_weight.shape[1]
    elec_size = lax.axis_size("elec")
    elec_total = elec_dev * elec_size
    walker_total = walkers_dev * lax.axis_size("walk")
    msg_scale = 1.0 / math.sqrt(elec_total)
    grad_scale = 1.0 / math.sqrt(walker_total * elec_total)
    filter_pairs = filter_weight.reshape(2 * basis_count, features)

    pos_t = jnp.transpose(positions, (0, 2, 1))
    hi = lax.reduce_precision(pos_t, exponent_bits=8, mantissa_bits=7)
    rest = pos_t - hi
    mid = lax.reduce_precision(rest, exponent_bits=8, mantissa_bits=7)
    pos_hi = hi.astype(jnp.bfloat16)
    pos_mid = mid.astype(jnp.bfloat16)
    pos_lo = (rest - mid).astype(jnp.bfloat16)
    spin_b = jnp.broadcast_to(spin_labels.astype(jnp.bfloat16)[None, :, None], (walkers_dev, elec_dev, 1))
    packed = jnp.concatenate([tokens, cotangent, pos_hi, pos_mid, pos_lo, spin_b], axis=-1)
    whole = lax.all_to_all(packed, "elec", 0, 0, tiled=True).reshape(elec_total, -1)
    walker_tok = whole[:, :features]
    walker_cot = whole[:, features : 2 * features]
    tail = whole[:, 2 * features :].astype(jnp.float32)
    walker_pos = (tail[:, 0:3] + tail[:, 3:6]) + tail[:, 6:9]
    spins = tail[:, 9]

    per_walker = walkers_dev // elec_size
    system = system_ids[lax.axis_index("elec") * per_walker]
    head_mat = lax.dynamic_index_in_dim(head_weight, system, 0, keepdims=False)

    msg_grads = jnp.dot(walker_cot, head_mat.T, preferred_element_type=jnp.float32).astype(jnp.bfloat16)
    tok_f = walker_tok.astype(jnp.float32)
    grads_f = msg_grads.astype(jnp.float32)

    spacing = cutoff_radius / (basis_count - 1)
    centers = jnp.arange(basis_count, dtype=jnp.float32) * spacing
    all_index = jnp.arange(elec_total, dtype=jnp.int32)
    block_rows = math.gcd(elec_total, 64)
    scaled_grads = msg_scale * grads_f

    def one_block(block_index, running):
        msg_out, back_out, weight_run = running
        first = block_index * block_rows
        near_pos = lax.dynamic_slice_in_dim(walker_pos, first, block_rows, 0)
        near_spin = lax.dynamic_slice_in_dim(spins, first, block_rows, 0)
        near_grads = lax.dynamic_slice_in_dim(scaled_grads, first, block_rows, 0)
        near_index = first + jnp.arange(block_rows, dtype=jnp.int32)
        offsets = near_pos[:, None, :] - walker_pos[None, :, :]
        squares = offsets * offsets
        distance = jnp.sqrt(squares[..., 0] + squares[..., 1] + squares[..., 2])
        radial = jnp.exp(-jnp.square((distance[..., None] - centers) / spacing))
        same_spin = (near_spin[:, None] == spins[None, :])[..., None]
        nothing = jnp.zeros_like(radial)
        pair_feats = jnp.concatenate(
            [jnp.where(same_spin, radial, nothing), jnp.where(same_spin, nothing, radial)], axis=-1
        ).astype(jnp.bfloat16)
        pre_act = jnp.einsum("ijk,kf->ijf", pair_feats, filter_pairs, preferred_element_type=jnp.float32)
        off_diag = (near_index[:, None] != all_index[None, :])[..., None]
        gate = logistic(pre_act)
        filters = jnp.where(off_diag, pre_act * gate, 0.0).astype(jnp.bfloat16).astype(jnp.float32)
        msg_rows = jnp.sum(filters * tok_f[None, :, :], axis=1)
        back_rows = jnp.sum(filters * grads_f[None, :, :], axis=1)
        slope = gate * (1.0 + pre_act * (1.0 - gate))
        pre_grad = near_grads[:, None, :] * tok_f[None, :, :] * slope
        pre_grad = jnp.where(off_diag, pre_grad, 0.0).astype(jnp.bfloat16)
        weight_run = weight_run + jnp.einsum(
            "ijk,ijf->kf", pair_feats, pre_grad, preferred_element_type=jnp.float32
        )
        msg_out = lax.dynamic_update_slice_in_dim(msg_out, msg_rows, first, 0)
        back_out = lax.dynamic_update_slice_in_dim(back_out, back_rows, first, 0)
        return (msg_out, back_out, weight_run)

    zero_rows = jnp.zeros((elec_total, features), jnp.float32)
    weight_zero = jnp.zeros((2 * basis_count, features), jnp.float32)
    msg_sum, back_sum, weight_sum = lax.fori_loop(
        0, elec_total // block_rows, one_block, (zero_rows, zero_rows, weight_zero)
    )

    messages = (msg_scale * msg_sum).astype(jnp.bfloat16)
    head_out = jnp.dot(messages, head_mat, preferred_element_type=jnp.float32)
    layer_out = (tok_f + head_out).astype(jnp.bfloat16)
    token_grad = walker_cot.astype(jnp.float32) + msg_scale * back_sum

    weight_total = butterfly_sum(weight_sum, ("walk", "elec"))
    filter_grad = (grad_scale * weight_total).reshape(2, basis_count, features)

    result = jnp.concatenate([layer_out.astype(jnp.float32), token_grad], axis=-1)
    result = lax.all_to_all(result.reshape(elec_size, elec_dev, -1), "elec", 0, 0, tiled=True)
    return (result[..., :features].astype(jnp.bfloat16), result[..., features:], filter_grad)


def solution(mesh):
    in_specs = (
        P("walk", "elec", None),
        P("walk", None, "elec"),
        P("elec"),
        P("walk"),
        P(),
        P(),
        P("walk", "elec", None),
    )
    out_specs = (P("walk", "elec", None), P("walk", "elec", None), P())
    return jax.shard_map(body, mesh=mesh, in_specs=in_specs, out_specs=out_specs, check_vma=False)
```

```python
import math

import jax
import jax.numpy as jnp
from jax import lax
from jax.sharding import PartitionSpec as P

cutoff_radius = 8.0


def logistic(values):
    return 0.5 * jnp.tanh(0.5 * values) + 0.5


def butterfly_sum(values, axes):
    for axis in axes:
        size = lax.axis_size(axis)
        step = 1
        while step < size:
            pairs = [(i, i ^ step) for i in range(size)]
            values = values + lax.ppermute(values, axis, pairs)
            step *= 2
    return values


def body(tokens, positions, spin_labels, system_ids, filter_weight, head_weight, cotangent):
    walkers_dev, elec_dev, features = tokens.shape
    basis_count = filter_weight.shape[1]
    elec_size = lax.axis_size("elec")
    elec_total = elec_dev * elec_size
    walker_total = walkers_dev * lax.axis_size("walk")
    msg_scale = 1.0 / math.sqrt(elec_total)
    grad_scale = 1.0 / math.sqrt(walker_total * elec_total)
    filter_pairs = filter_weight.reshape(2 * basis_count, features)

    pos_t = jnp.transpose(positions, (0, 2, 1))
    hi = lax.reduce_precision(pos_t, exponent_bits=8, mantissa_bits=7)
    rest = pos_t - hi
    mid = lax.reduce_precision(rest, exponent_bits=8, mantissa_bits=7)
    pos_hi = hi.astype(jnp.bfloat16)
    pos_mid = mid.astype(jnp.bfloat16)
    pos_lo = (rest - mid).astype(jnp.bfloat16)
    spin_b = jnp.broadcast_to(spin_labels.astype(jnp.bfloat16)[None, :, None], (walkers_dev, elec_dev, 1))
    packed = jnp.concatenate([tokens, cotangent, pos_hi, pos_mid, pos_lo, spin_b], axis=-1)
    whole = lax.all_to_all(packed, "elec", 0, 0, tiled=True).reshape(elec_total, -1)
    walker_tok = whole[:, :features]
    walker_cot = whole[:, features : 2 * features]
    tail = whole[:, 2 * features :].astype(jnp.float32)
    walker_pos = (tail[:, 0:3] + tail[:, 3:6]) + tail[:, 6:9]
    spins = tail[:, 9]

    per_walker = walkers_dev // elec_size
    system = system_ids[lax.axis_index("elec") * per_walker]
    head_mat = lax.dynamic_index_in_dim(head_weight, system, 0, keepdims=False)

    msg_grads = jnp.dot(walker_cot, head_mat.T, preferred_element_type=jnp.float32).astype(jnp.bfloat16)
    tok_f = walker_tok.astype(jnp.float32)
    grads_f = msg_grads.astype(jnp.float32)

    spacing = cutoff_radius / (basis_count - 1)
    centers = jnp.arange(basis_count, dtype=jnp.float32) * spacing
    all_index = jnp.arange(elec_total, dtype=jnp.int32)
    block_rows = math.gcd(elec_total, 64)
    scaled_grads = msg_scale * grads_f

    block_count = elec_total // block_rows

    def block_terms(first):
        near_pos = lax.dynamic_slice_in_dim(walker_pos, first, block_rows, 0)
        near_spin = lax.dynamic_slice_in_dim(spins, first, block_rows, 0)
        near_index = first + jnp.arange(block_rows, dtype=jnp.int32)
        offsets = near_pos[:, None, :] - walker_pos[None, :, :]
        squares = offsets * offsets
        distance = jnp.sqrt(squares[..., 0] + squares[..., 1] + squares[..., 2])
        radial = jnp.exp(-jnp.square((distance[..., None] - centers) / spacing))
        same_spin = (near_spin[:, None] == spins[None, :])[..., None]
        nothing = jnp.zeros_like(radial)
        pair_feats = jnp.concatenate(
            [jnp.where(same_spin, radial, nothing), jnp.where(same_spin, nothing, radial)], axis=-1
        ).astype(jnp.bfloat16)
        pre_act = jnp.einsum("ijk,kf->ijf", pair_feats, filter_pairs, preferred_element_type=jnp.float32)
        off_diag = (near_index[:, None] != all_index[None, :])[..., None]
        return pair_feats, pre_act, logistic(pre_act), off_diag

    def weight_block(block_index, weight_run):
        first = block_index * block_rows
        pair_feats, pre_act, gate, off_diag = block_terms(first)
        near_grads = lax.dynamic_slice_in_dim(scaled_grads, first, block_rows, 0)
        slope = gate * (1.0 + pre_act * (1.0 - gate))
        pre_grad = near_grads[:, None, :] * tok_f[None, :, :] * slope
        pre_grad = jnp.where(off_diag, pre_grad, 0.0).astype(jnp.bfloat16)
        return weight_run + jnp.einsum("ijk,ijf->kf", pair_feats, pre_grad, preferred_element_type=jnp.float32)

    def message_block(first, tok_all, grads_all):
        unused_feats, pre_act, gate, off_diag = block_terms(first)
        filters = jnp.where(off_diag, pre_act * gate, 0.0).astype(jnp.bfloat16).astype(jnp.float32)
        return (jnp.sum(filters * tok_all[None, :, :], axis=1), jnp.sum(filters * grads_all[None, :, :], axis=1))

    weight_zero = jnp.zeros((2 * basis_count, features), jnp.float32)
    weight_sum = lax.fori_loop(0, block_count, weight_block, weight_zero)

    values = weight_sum
    msg_parts, back_parts = [], []
    done = 0
    for axis in ("walk", "elec"):
        size = lax.axis_size(axis)
        step = 1
        while step < size:
            pairs = [(i, i ^ step) for i in range(size)]
            if done < block_count:
                values, tok_b, grads_b = lax.optimization_barrier((values, tok_f, grads_f))
                arrived = lax.ppermute(values, axis, pairs)
                msg_rows, back_rows = message_block(done * block_rows, tok_b, grads_b)
                arrived, msg_rows, back_rows = lax.optimization_barrier((arrived, msg_rows, back_rows))
                msg_parts.append(msg_rows)
                back_parts.append(back_rows)
            else:
                arrived = lax.ppermute(values, axis, pairs)
            values = values + arrived
            step *= 2
            done += 1
    weight_total = values
    msg_sum = jnp.concatenate(msg_parts, axis=0)
    back_sum = jnp.concatenate(back_parts, axis=0)

    messages = (msg_scale * msg_sum).astype(jnp.bfloat16)
    head_out = jnp.dot(messages, head_mat, preferred_element_type=jnp.float32)
    layer_out = (tok_f + head_out).astype(jnp.bfloat16)
    token_grad = walker_cot.astype(jnp.float32) + msg_scale * back_sum

    filter_grad = (grad_scale * weight_total).reshape(2, basis_count, features)

    result = jnp.concatenate([layer_out.astype(jnp.float32), token_grad], axis=-1)
    result = lax.all_to_all(result.reshape(elec_size, elec_dev, -1), "elec", 0, 0, tiled=True)
    return (result[..., :features].astype(jnp.bfloat16), result[..., features:], filter_grad)


def solution(mesh):
    in_specs = (
        P("walk", "elec", None),
        P("walk", None, "elec"),
        P("elec"),
        P("walk"),
        P(),
        P(),
        P("walk", "elec", None),
    )
    out_specs = (P("walk", "elec", None), P("walk", "elec", None), P())
    return jax.shard_map(body, mesh=mesh, in_specs=in_specs, out_specs=out_specs, check_vma=False)
```

```python
import math

import jax
import jax.numpy as jnp
from jax import lax
from jax.sharding import PartitionSpec as P

cutoff_radius = 8.0


def logistic(values):
    return 0.5 * jnp.tanh(0.5 * values) + 0.5


def butterfly_sum(values, axes):
    for axis in axes:
        size = lax.axis_size(axis)
        step = 1
        while step < size:
            pairs = [(i, i ^ step) for i in range(size)]
            values = values + lax.ppermute(values, axis, pairs)
            step *= 2
    return values


def body(tokens, positions, spin_labels, system_ids, filter_weight, head_weight, cotangent):
    walkers_dev, elec_dev, features = tokens.shape
    basis_count = filter_weight.shape[1]
    elec_size = lax.axis_size("elec")
    elec_total = elec_dev * elec_size
    walker_total = walkers_dev * lax.axis_size("walk")
    msg_scale = 1.0 / math.sqrt(elec_total)
    grad_scale = 1.0 / math.sqrt(walker_total * elec_total)
    filter_pairs = filter_weight.reshape(2 * basis_count, features)

    pos_t = jnp.transpose(positions, (0, 2, 1))
    hi = lax.reduce_precision(pos_t, exponent_bits=8, mantissa_bits=7)
    rest = pos_t - hi
    mid = lax.reduce_precision(rest, exponent_bits=8, mantissa_bits=7)
    pos_hi = hi.astype(jnp.bfloat16)
    pos_mid = mid.astype(jnp.bfloat16)
    pos_lo = (rest - mid).astype(jnp.bfloat16)
    spin_b = jnp.broadcast_to(spin_labels.astype(jnp.bfloat16)[None, :, None], (walkers_dev, elec_dev, 1))
    packed = jnp.concatenate([tokens, cotangent, pos_hi, pos_mid, pos_lo, spin_b], axis=-1)
    whole = lax.all_to_all(packed, "elec", 0, 0, tiled=True).reshape(elec_total, -1)
    walker_tok = whole[:, :features]
    walker_cot = whole[:, features : 2 * features]
    tail = whole[:, 2 * features :].astype(jnp.float32)
    walker_pos = (tail[:, 0:3] + tail[:, 3:6]) + tail[:, 6:9]
    spins = tail[:, 9]

    per_walker = walkers_dev // elec_size
    system = system_ids[lax.axis_index("elec") * per_walker]
    head_mat = lax.dynamic_index_in_dim(head_weight, system, 0, keepdims=False)

    msg_grads = jnp.dot(walker_cot, head_mat.T, preferred_element_type=jnp.float32).astype(jnp.bfloat16)
    tok_f = walker_tok.astype(jnp.float32)
    grads_f = msg_grads.astype(jnp.float32)

    spacing = cutoff_radius / (basis_count - 1)
    centers = jnp.arange(basis_count, dtype=jnp.float32) * spacing
    all_index = jnp.arange(elec_total, dtype=jnp.int32)
    block_rows = math.gcd(elec_total, 64)
    scaled_grads = msg_scale * grads_f

    block_count = elec_total // block_rows

    def block_terms(first):
        near_pos = lax.dynamic_slice_in_dim(walker_pos, first, block_rows, 0)
        near_spin = lax.dynamic_slice_in_dim(spins, first, block_rows, 0)
        near_index = first + jnp.arange(block_rows, dtype=jnp.int32)
        offsets = near_pos[:, None, :] - walker_pos[None, :, :]
        squares = offsets * offsets
        distance = jnp.sqrt(squares[..., 0] + squares[..., 1] + squares[..., 2])
        radial = jnp.exp(-jnp.square((distance[..., None] - centers) / spacing))
        same_spin = (near_spin[:, None] == spins[None, :])[..., None]
        nothing = jnp.zeros_like(radial)
        pair_feats = jnp.concatenate(
            [jnp.where(same_spin, radial, nothing), jnp.where(same_spin, nothing, radial)], axis=-1
        ).astype(jnp.bfloat16)
        pre_act = jnp.einsum("ijk,kf->ijf", pair_feats, filter_pairs, preferred_element_type=jnp.float32)
        off_diag = (near_index[:, None] != all_index[None, :])[..., None]
        return pair_feats, pre_act, logistic(pre_act), off_diag

    def weight_block(block_index, weight_run):
        first = block_index * block_rows
        pair_feats, pre_act, gate, off_diag = block_terms(first)
        near_grads = lax.dynamic_slice_in_dim(scaled_grads, first, block_rows, 0)
        slope = gate * (1.0 + pre_act * (1.0 - gate))
        pre_grad = near_grads[:, None, :] * tok_f[None, :, :] * slope
        pre_grad = jnp.where(off_diag, pre_grad, 0.0).astype(jnp.bfloat16)
        return weight_run + jnp.einsum("ijk,ijf->kf", pair_feats, pre_grad, preferred_element_type=jnp.float32)

    def message_block(first, tok_all, grads_all):
        unused_feats, pre_act, gate, off_diag = block_terms(first)
        filters = jnp.where(off_diag, pre_act * gate, 0.0).astype(jnp.bfloat16).astype(jnp.float32)
        return (jnp.sum(filters * tok_all[None, :, :], axis=1), jnp.sum(filters * grads_all[None, :, :], axis=1))

    weight_zero = jnp.zeros((2 * basis_count, features), jnp.float32)
    weight_sum = lax.fori_loop(0, block_count, weight_block, weight_zero)

    values = weight_sum
    msg_parts, back_parts = [], []
    walk_size, elec_size_ = lax.axis_size("walk"), lax.axis_size("elec")
    order = [("walk", 1), ("walk", 2)]
    order += [("elec", 1 << b) for b in range(max(elec_size_.bit_length() - 2, 0))]
    order += [("walk", 1 << b) for b in range(2, walk_size.bit_length() - 1)]
    order += [("elec", elec_size_ // 2)]
    for done, (axis, step) in enumerate(order):
        size = lax.axis_size(axis)
        pairs = [(i, i ^ step) for i in range(size)]
        if done < block_count:
            values, tok_b, grads_b = lax.optimization_barrier((values, tok_f, grads_f))
            arrived = lax.ppermute(values, axis, pairs)
            msg_rows, back_rows = message_block(done * block_rows, tok_b, grads_b)
            arrived, msg_rows, back_rows = lax.optimization_barrier((arrived, msg_rows, back_rows))
            msg_parts.append(msg_rows)
            back_parts.append(back_rows)
        else:
            arrived = lax.ppermute(values, axis, pairs)
        values = values + arrived
    weight_total = values
    msg_sum = jnp.concatenate(msg_parts, axis=0)
    back_sum = jnp.concatenate(back_parts, axis=0)

    messages = (msg_scale * msg_sum).astype(jnp.bfloat16)
    head_out = jnp.dot(messages, head_mat, preferred_element_type=jnp.float32)
    layer_out = (tok_f + head_out).astype(jnp.bfloat16)
    token_grad = walker_cot.astype(jnp.float32) + msg_scale * back_sum

    filter_grad = (grad_scale * weight_total).reshape(2, basis_count, features)

    result = jnp.concatenate([layer_out.astype(jnp.float32), token_grad], axis=-1)
    result = lax.all_to_all(result.reshape(elec_size, elec_dev, -1), "elec", 0, 0, tiled=True)
    return (result[..., :features].astype(jnp.bfloat16), result[..., features:], filter_grad)


def solution(mesh):
    in_specs = (
        P("walk", "elec", None),
        P("walk", None, "elec"),
        P("elec"),
        P("walk"),
        P(),
        P(),
        P("walk", "elec", None),
    )
    out_specs = (P("walk", "elec", None), P("walk", "elec", None), P())
    return jax.shard_map(body, mesh=mesh, in_specs=in_specs, out_specs=out_specs, check_vma=False)
```

```python
import math

import jax
import jax.numpy as jnp
from jax import lax
from jax.sharding import PartitionSpec as P

cutoff_radius = 8.0


def logistic(values):
    return 0.5 * jnp.tanh(0.5 * values) + 0.5


def butterfly_sum(values, axes):
    for axis in axes:
        size = lax.axis_size(axis)
        step = 1
        while step < size:
            pairs = [(i, i ^ step) for i in range(size)]
            values = values + lax.ppermute(values, axis, pairs)
            step *= 2
    return values


def body(tokens, positions, spin_labels, system_ids, filter_weight, head_weight, cotangent):
    walkers_dev, elec_dev, features = tokens.shape
    basis_count = filter_weight.shape[1]
    elec_size = lax.axis_size("elec")
    elec_total = elec_dev * elec_size
    walker_total = walkers_dev * lax.axis_size("walk")
    msg_scale = 1.0 / math.sqrt(elec_total)
    grad_scale = 1.0 / math.sqrt(walker_total * elec_total)
    filter_pairs = filter_weight.reshape(2 * basis_count, features)

    pos_t = jnp.transpose(positions, (0, 2, 1))
    hi = lax.reduce_precision(pos_t, exponent_bits=8, mantissa_bits=7)
    rest = pos_t - hi
    mid = lax.reduce_precision(rest, exponent_bits=8, mantissa_bits=7)
    pos_hi = hi.astype(jnp.bfloat16)
    pos_mid = mid.astype(jnp.bfloat16)
    pos_lo = (rest - mid).astype(jnp.bfloat16)
    spin_b = jnp.broadcast_to(spin_labels.astype(jnp.bfloat16)[None, :, None], (walkers_dev, elec_dev, 1))
    packed = jnp.concatenate([tokens, cotangent, pos_hi, pos_mid, pos_lo, spin_b], axis=-1)
    whole = lax.all_to_all(packed, "elec", 0, 0, tiled=True).reshape(elec_total, -1)
    walker_tok = whole[:, :features]
    walker_cot = whole[:, features : 2 * features]
    tail = whole[:, 2 * features :].astype(jnp.float32)
    walker_pos = (tail[:, 0:3] + tail[:, 3:6]) + tail[:, 6:9]
    spins = tail[:, 9]

    per_walker = walkers_dev // elec_size
    system = system_ids[lax.axis_index("elec") * per_walker]
    head_mat = lax.dynamic_index_in_dim(head_weight, system, 0, keepdims=False)

    msg_grads = jnp.dot(walker_cot, head_mat.T, preferred_element_type=jnp.float32).astype(jnp.bfloat16)
    tok_f = walker_tok.astype(jnp.float32)
    grads_f = msg_grads.astype(jnp.float32)

    spacing = cutoff_radius / (basis_count - 1)
    centers = jnp.arange(basis_count, dtype=jnp.float32) * spacing
    all_index = jnp.arange(elec_total, dtype=jnp.int32)
    block_rows = math.gcd(elec_total, 64)
    scaled_grads = msg_scale * grads_f

    block_count = elec_total // block_rows

    def block_terms(first, rows=block_rows):
        near_pos = lax.dynamic_slice_in_dim(walker_pos, first, rows, 0)
        near_spin = lax.dynamic_slice_in_dim(spins, first, rows, 0)
        near_index = first + jnp.arange(rows, dtype=jnp.int32)
        offsets = near_pos[:, None, :] - walker_pos[None, :, :]
        squares = offsets * offsets
        distance = jnp.sqrt(squares[..., 0] + squares[..., 1] + squares[..., 2])
        radial = jnp.exp(-jnp.square((distance[..., None] - centers) / spacing))
        same_spin = (near_spin[:, None] == spins[None, :])[..., None]
        nothing = jnp.zeros_like(radial)
        pair_feats = jnp.concatenate(
            [jnp.where(same_spin, radial, nothing), jnp.where(same_spin, nothing, radial)], axis=-1
        ).astype(jnp.bfloat16)
        pre_act = jnp.einsum("ijk,kf->ijf", pair_feats, filter_pairs, preferred_element_type=jnp.float32)
        off_diag = (near_index[:, None] != all_index[None, :])[..., None]
        return pair_feats, pre_act, logistic(pre_act), off_diag

    def weight_block(block_index, weight_run):
        first = block_index * block_rows
        pair_feats, pre_act, gate, off_diag = block_terms(first)
        near_grads = lax.dynamic_slice_in_dim(scaled_grads, first, block_rows, 0)
        slope = gate * (1.0 + pre_act * (1.0 - gate))
        pre_grad = near_grads[:, None, :] * tok_f[None, :, :] * slope
        pre_grad = jnp.where(off_diag, pre_grad, 0.0).astype(jnp.bfloat16)
        return weight_run + jnp.einsum("ijk,ijf->kf", pair_feats, pre_grad, preferred_element_type=jnp.float32)

    message_rows = math.gcd(elec_total, 32)
    message_count = elec_total // message_rows

    def message_block(first, tok_all, grads_all):
        unused_feats, pre_act, gate, off_diag = block_terms(first, message_rows)
        filters = jnp.where(off_diag, pre_act * gate, 0.0).astype(jnp.bfloat16).astype(jnp.float32)
        return (jnp.sum(filters * tok_all[None, :, :], axis=1), jnp.sum(filters * grads_all[None, :, :], axis=1))

    weight_zero = jnp.zeros((2 * basis_count, features), jnp.float32)
    weight_sum = lax.fori_loop(0, block_count, weight_block, weight_zero)

    values = weight_sum
    msg_parts, back_parts = [], []
    walk_size, elec_size_ = lax.axis_size("walk"), lax.axis_size("elec")
    order = [("walk", 1), ("walk", 2)]
    order += [("elec", 1 << b) for b in range(max(elec_size_.bit_length() - 2, 0))]
    order += [("walk", 1 << b) for b in range(2, walk_size.bit_length() - 1)]
    order += [("elec", elec_size_ // 2)]
    for done, (axis, step) in enumerate(order):
        size = lax.axis_size(axis)
        pairs = [(i, i ^ step) for i in range(size)]
        if done < message_count:
            values, tok_b, grads_b = lax.optimization_barrier((values, tok_f, grads_f))
            arrived = lax.ppermute(values, axis, pairs)
            msg_rows, back_rows = message_block(done * message_rows, tok_b, grads_b)
            arrived, msg_rows, back_rows = lax.optimization_barrier((arrived, msg_rows, back_rows))
            msg_parts.append(msg_rows)
            back_parts.append(back_rows)
        else:
            arrived = lax.ppermute(values, axis, pairs)
        values = values + arrived
    weight_total = values
    msg_sum = jnp.concatenate(msg_parts, axis=0)
    back_sum = jnp.concatenate(back_parts, axis=0)

    messages = (msg_scale * msg_sum).astype(jnp.bfloat16)
    head_out = jnp.dot(messages, head_mat, preferred_element_type=jnp.float32)
    layer_out = (tok_f + head_out).astype(jnp.bfloat16)
    token_grad = walker_cot.astype(jnp.float32) + msg_scale * back_sum

    filter_grad = (grad_scale * weight_total).reshape(2, basis_count, features)

    result = jnp.concatenate([layer_out.astype(jnp.float32), token_grad], axis=-1)
    result = lax.all_to_all(result.reshape(elec_size, elec_dev, -1), "elec", 0, 0, tiled=True)
    return (result[..., :features].astype(jnp.bfloat16), result[..., features:], filter_grad)


def solution(mesh):
    in_specs = (
        P("walk", "elec", None),
        P("walk", None, "elec"),
        P("elec"),
        P("walk"),
        P(),
        P(),
        P("walk", "elec", None),
    )
    out_specs = (P("walk", "elec", None), P("walk", "elec", None), P())
    return jax.shard_map(body, mesh=mesh, in_specs=in_specs, out_specs=out_specs, check_vma=False)
```

```python
import math

import jax
import jax.numpy as jnp
from jax import lax
from jax.sharding import PartitionSpec as P

cutoff_radius = 8.0


def logistic(values):
    return 0.5 * jnp.tanh(0.5 * values) + 0.5


def butterfly_sum(values, axes):
    for axis in axes:
        size = lax.axis_size(axis)
        step = 1
        while step < size:
            pairs = [(i, i ^ step) for i in range(size)]
            values = values + lax.ppermute(values, axis, pairs)
            step *= 2
    return values


def body(tokens, positions, spin_labels, system_ids, filter_weight, head_weight, cotangent):
    walkers_dev, elec_dev, features = tokens.shape
    basis_count = filter_weight.shape[1]
    elec_size = lax.axis_size("elec")
    elec_total = elec_dev * elec_size
    walker_total = walkers_dev * lax.axis_size("walk")
    msg_scale = 1.0 / math.sqrt(elec_total)
    grad_scale = 1.0 / math.sqrt(walker_total * elec_total)
    filter_pairs = filter_weight.reshape(2 * basis_count, features)

    pos_t = jnp.transpose(positions, (0, 2, 1))
    hi = lax.reduce_precision(pos_t, exponent_bits=8, mantissa_bits=7)
    rest = pos_t - hi
    mid = lax.reduce_precision(rest, exponent_bits=8, mantissa_bits=7)
    pos_hi = hi.astype(jnp.bfloat16)
    pos_mid = mid.astype(jnp.bfloat16)
    pos_lo = (rest - mid).astype(jnp.bfloat16)
    spin_b = jnp.broadcast_to(spin_labels.astype(jnp.bfloat16)[None, :, None], (walkers_dev, elec_dev, 1))
    packed = jnp.concatenate([tokens, cotangent, pos_hi, pos_mid, pos_lo, spin_b], axis=-1)
    whole = lax.all_to_all(packed, "elec", 0, 0, tiled=True).reshape(elec_total, -1)
    walker_tok = whole[:, :features]
    walker_cot = whole[:, features : 2 * features]
    tail = whole[:, 2 * features :].astype(jnp.float32)
    walker_pos = (tail[:, 0:3] + tail[:, 3:6]) + tail[:, 6:9]
    spins = tail[:, 9]

    per_walker = walkers_dev // elec_size
    system = system_ids[lax.axis_index("elec") * per_walker]
    head_mat = lax.dynamic_index_in_dim(head_weight, system, 0, keepdims=False)

    msg_grads = jnp.dot(walker_cot, head_mat.T, preferred_element_type=jnp.float32).astype(jnp.bfloat16)
    tok_f = walker_tok.astype(jnp.float32)
    grads_f = msg_grads.astype(jnp.float32)

    spacing = cutoff_radius / (basis_count - 1)
    centers = jnp.arange(basis_count, dtype=jnp.float32) * spacing
    all_index = jnp.arange(elec_total, dtype=jnp.int32)
    block_rows = math.gcd(elec_total, 64)
    scaled_grads = msg_scale * grads_f

    block_count = elec_total // block_rows

    def block_terms(first):
        near_pos = lax.dynamic_slice_in_dim(walker_pos, first, block_rows, 0)
        near_spin = lax.dynamic_slice_in_dim(spins, first, block_rows, 0)
        near_index = first + jnp.arange(block_rows, dtype=jnp.int32)
        offsets = near_pos[:, None, :] - walker_pos[None, :, :]
        squares = offsets * offsets
        distance = jnp.sqrt(squares[..., 0] + squares[..., 1] + squares[..., 2])
        radial = jnp.exp(-jnp.square((distance[..., None] - centers) / spacing))
        same_spin = (near_spin[:, None] == spins[None, :])[..., None]
        nothing = jnp.zeros_like(radial)
        pair_feats = jnp.concatenate(
            [jnp.where(same_spin, radial, nothing), jnp.where(same_spin, nothing, radial)], axis=-1
        ).astype(jnp.bfloat16)
        pre_act = jnp.einsum("ijk,kf->ijf", pair_feats, filter_pairs, preferred_element_type=jnp.float32)
        off_diag = (near_index[:, None] != all_index[None, :])[..., None]
        return pair_feats, pre_act, logistic(pre_act), off_diag

    def weight_block(block_index, weight_run):
        first = block_index * block_rows
        pair_feats, pre_act, gate, off_diag = block_terms(first)
        near_grads = lax.dynamic_slice_in_dim(scaled_grads, first, block_rows, 0)
        slope = gate * (1.0 + pre_act * (1.0 - gate))
        pre_grad = near_grads[:, None, :] * tok_f[None, :, :] * slope
        pre_grad = jnp.where(off_diag, pre_grad, 0.0).astype(jnp.bfloat16)
        return weight_run + jnp.einsum("ijk,ijf->kf", pair_feats, pre_grad, preferred_element_type=jnp.float32)

    def message_block(first, tok_all, grads_all):
        unused_feats, pre_act, gate, off_diag = block_terms(first)
        filters = jnp.where(off_diag, pre_act * gate, 0.0).astype(jnp.bfloat16).astype(jnp.float32)
        return (jnp.sum(filters * tok_all[None, :, :], axis=1), jnp.sum(filters * grads_all[None, :, :], axis=1))

    weight_zero = jnp.zeros((2 * basis_count, features), jnp.float32)
    weight_sum = lax.fori_loop(0, block_count, weight_block, weight_zero)

    values = weight_sum
    msg_parts, back_parts = [], []
    walk_size, elec_size_ = lax.axis_size("walk"), lax.axis_size("elec")
    order = [("walk", 1), ("walk", 2)]
    order += [("elec", 1 << b) for b in range(max(elec_size_.bit_length() - 2, 0))]
    order += [("elec", elec_size_ // 2)]
    order += [("walk", 1 << b) for b in range(2, walk_size.bit_length() - 1)]
    for done, (axis, step) in enumerate(order):
        size = lax.axis_size(axis)
        pairs = [(i, i ^ step) for i in range(size)]
        if done < block_count:
            values, tok_b, grads_b = lax.optimization_barrier((values, tok_f, grads_f))
            arrived = lax.ppermute(values, axis, pairs)
            msg_rows, back_rows = message_block(done * block_rows, tok_b, grads_b)
            arrived, msg_rows, back_rows = lax.optimization_barrier((arrived, msg_rows, back_rows))
            msg_parts.append(msg_rows)
            back_parts.append(back_rows)
        else:
            arrived = lax.ppermute(values, axis, pairs)
        values = values + arrived
    weight_total = values
    msg_sum = jnp.concatenate(msg_parts, axis=0)
    back_sum = jnp.concatenate(back_parts, axis=0)

    messages = (msg_scale * msg_sum).astype(jnp.bfloat16)
    head_out = jnp.dot(messages, head_mat, preferred_element_type=jnp.float32)
    layer_out = (tok_f + head_out).astype(jnp.bfloat16)
    token_grad = walker_cot.astype(jnp.float32) + msg_scale * back_sum

    filter_grad = (grad_scale * weight_total).reshape(2, basis_count, features)

    result = jnp.concatenate([layer_out.astype(jnp.float32), token_grad], axis=-1)
    result = lax.all_to_all(result.reshape(elec_size, elec_dev, -1), "elec", 0, 0, tiled=True)
    return (result[..., :features].astype(jnp.bfloat16), result[..., features:], filter_grad)


def solution(mesh):
    in_specs = (
        P("walk", "elec", None),
        P("walk", None, "elec"),
        P("elec"),
        P("walk"),
        P(),
        P(),
        P("walk", "elec", None),
    )
    out_specs = (P("walk", "elec", None), P("walk", "elec", None), P())
    return jax.shard_map(body, mesh=mesh, in_specs=in_specs, out_specs=out_specs, check_vma=False)
```

```python
import math

import jax
import jax.numpy as jnp
from jax import lax
from jax.sharding import PartitionSpec as P

cutoff_radius = 8.0


def logistic(values):
    return 0.5 * jnp.tanh(0.5 * values) + 0.5


def butterfly_sum(values, axes):
    for axis in axes:
        size = lax.axis_size(axis)
        step = 1
        while step < size:
            pairs = [(i, i ^ step) for i in range(size)]
            values = values + lax.ppermute(values, axis, pairs)
            step *= 2
    return values


def body(tokens, positions, spin_labels, system_ids, filter_weight, head_weight, cotangent):
    walkers_dev, elec_dev, features = tokens.shape
    basis_count = filter_weight.shape[1]
    elec_size = lax.axis_size("elec")
    elec_total = elec_dev * elec_size
    walker_total = walkers_dev * lax.axis_size("walk")
    msg_scale = 1.0 / math.sqrt(elec_total)
    grad_scale = 1.0 / math.sqrt(walker_total * elec_total)
    filter_pairs = filter_weight.reshape(2 * basis_count, features)

    pos_t = jnp.transpose(positions, (0, 2, 1))
    hi = lax.reduce_precision(pos_t, exponent_bits=8, mantissa_bits=7)
    rest = pos_t - hi
    mid = lax.reduce_precision(rest, exponent_bits=8, mantissa_bits=7)
    pos_hi = hi.astype(jnp.bfloat16)
    pos_mid = mid.astype(jnp.bfloat16)
    pos_lo = (rest - mid).astype(jnp.bfloat16)
    spin_b = jnp.broadcast_to(spin_labels.astype(jnp.bfloat16)[None, :, None], (walkers_dev, elec_dev, 1))
    packed = jnp.concatenate([tokens, cotangent, pos_hi, pos_mid, pos_lo, spin_b], axis=-1)
    whole = lax.all_to_all(packed, "elec", 0, 0, tiled=True).reshape(elec_total, -1)
    walker_tok = whole[:, :features]
    walker_cot = whole[:, features : 2 * features]
    tail = whole[:, 2 * features :].astype(jnp.float32)
    walker_pos = (tail[:, 0:3] + tail[:, 3:6]) + tail[:, 6:9]
    spins = tail[:, 9]

    per_walker = walkers_dev // elec_size
    system = system_ids[lax.axis_index("elec") * per_walker]
    head_mat = lax.dynamic_index_in_dim(head_weight, system, 0, keepdims=False)

    msg_grads = jnp.dot(walker_cot, head_mat.T, preferred_element_type=jnp.float32).astype(jnp.bfloat16)
    tok_f = walker_tok.astype(jnp.float32)
    grads_f = msg_grads.astype(jnp.float32)

    spacing = cutoff_radius / (basis_count - 1)
    centers = jnp.arange(basis_count, dtype=jnp.float32) * spacing
    all_index = jnp.arange(elec_total, dtype=jnp.int32)
    block_rows = math.gcd(elec_total, 64)
    scaled_grads = msg_scale * grads_f

    block_count = elec_total // block_rows

    def block_terms(first):
        near_pos = lax.dynamic_slice_in_dim(walker_pos, first, block_rows, 0)
        near_spin = lax.dynamic_slice_in_dim(spins, first, block_rows, 0)
        near_index = first + jnp.arange(block_rows, dtype=jnp.int32)
        offsets = near_pos[:, None, :] - walker_pos[None, :, :]
        squares = offsets * offsets
        distance = jnp.sqrt(squares[..., 0] + squares[..., 1] + squares[..., 2])
        radial = jnp.exp(-jnp.square((distance[..., None] - centers) / spacing))
        same_spin = (near_spin[:, None] == spins[None, :])[..., None]
        nothing = jnp.zeros_like(radial)
        pair_feats = jnp.concatenate(
            [jnp.where(same_spin, radial, nothing), jnp.where(same_spin, nothing, radial)], axis=-1
        ).astype(jnp.bfloat16)
        pre_act = jnp.einsum("ijk,kf->ijf", pair_feats, filter_pairs, preferred_element_type=jnp.float32)
        off_diag = (near_index[:, None] != all_index[None, :])[..., None]
        return pair_feats, pre_act, logistic(pre_act), off_diag

    def weight_block(block_index, weight_run):
        first = block_index * block_rows
        pair_feats, pre_act, gate, off_diag = block_terms(first)
        near_grads = lax.dynamic_slice_in_dim(scaled_grads, first, block_rows, 0)
        slope = gate * (1.0 + pre_act * (1.0 - gate))
        pre_grad = near_grads[:, None, :] * tok_f[None, :, :] * slope
        pre_grad = jnp.where(off_diag, pre_grad, 0.0).astype(jnp.bfloat16)
        return weight_run + jnp.einsum("ijk,ijf->kf", pair_feats, pre_grad, preferred_element_type=jnp.float32)

    def message_block(first, tok_all, grads_all):
        unused_feats, pre_act, gate, off_diag = block_terms(first)
        filters = jnp.where(off_diag, pre_act * gate, 0.0).astype(jnp.bfloat16).astype(jnp.float32)
        return (jnp.sum(filters * tok_all[None, :, :], axis=1), jnp.sum(filters * grads_all[None, :, :], axis=1))

    weight_zero = jnp.zeros((2 * basis_count, features), jnp.float32)
    weight_sum = lax.fori_loop(0, block_count, weight_block, weight_zero)

    values = weight_sum
    msg_parts, back_parts = [], []
    walk_size, elec_size_ = lax.axis_size("walk"), lax.axis_size("elec")
    order = [("walk", 1), ("walk", 2), ("elec", elec_size_ // 2)]
    order += [("elec", 1 << b) for b in range(max(elec_size_.bit_length() - 2, 0))]
    order += [("walk", 1 << b) for b in range(2, walk_size.bit_length() - 1)]
    for done, (axis, step) in enumerate(order):
        size = lax.axis_size(axis)
        pairs = [(i, i ^ step) for i in range(size)]
        if done < block_count:
            values, tok_b, grads_b = lax.optimization_barrier((values, tok_f, grads_f))
            arrived = lax.ppermute(values, axis, pairs)
            msg_rows, back_rows = message_block(done * block_rows, tok_b, grads_b)
            arrived, msg_rows, back_rows = lax.optimization_barrier((arrived, msg_rows, back_rows))
            msg_parts.append(msg_rows)
            back_parts.append(back_rows)
        else:
            arrived = lax.ppermute(values, axis, pairs)
        values = values + arrived
    weight_total = values
    msg_sum = jnp.concatenate(msg_parts, axis=0)
    back_sum = jnp.concatenate(back_parts, axis=0)

    messages = (msg_scale * msg_sum).astype(jnp.bfloat16)
    head_out = jnp.dot(messages, head_mat, preferred_element_type=jnp.float32)
    layer_out = (tok_f + head_out).astype(jnp.bfloat16)
    token_grad = walker_cot.astype(jnp.float32) + msg_scale * back_sum

    filter_grad = (grad_scale * weight_total).reshape(2, basis_count, features)

    result = jnp.concatenate([layer_out.astype(jnp.float32), token_grad], axis=-1)
    result = lax.all_to_all(result.reshape(elec_size, elec_dev, -1), "elec", 0, 0, tiled=True)
    return (result[..., :features].astype(jnp.bfloat16), result[..., features:], filter_grad)


def solution(mesh):
    in_specs = (
        P("walk", "elec", None),
        P("walk", None, "elec"),
        P("elec"),
        P("walk"),
        P(),
        P(),
        P("walk", "elec", None),
    )
    out_specs = (P("walk", "elec", None), P("walk", "elec", None), P())
    return jax.shard_map(body, mesh=mesh, in_specs=in_specs, out_specs=out_specs, check_vma=False)
```

```python
import math

import jax
import jax.numpy as jnp
from jax import lax
from jax.sharding import PartitionSpec as P

cutoff_radius = 8.0


def logistic(values):
    return 0.5 * jnp.tanh(0.5 * values) + 0.5


def butterfly_sum(values, axes):
    for axis in axes:
        size = lax.axis_size(axis)
        step = 1
        while step < size:
            pairs = [(i, i ^ step) for i in range(size)]
            values = values + lax.ppermute(values, axis, pairs)
            step *= 2
    return values


def body(tokens, positions, spin_labels, system_ids, filter_weight, head_weight, cotangent):
    walkers_dev, elec_dev, features = tokens.shape
    basis_count = filter_weight.shape[1]
    elec_size = lax.axis_size("elec")
    elec_total = elec_dev * elec_size
    walker_total = walkers_dev * lax.axis_size("walk")
    msg_scale = 1.0 / math.sqrt(elec_total)
    grad_scale = 1.0 / math.sqrt(walker_total * elec_total)
    filter_pairs = filter_weight.reshape(2 * basis_count, features)

    pos_t = jnp.transpose(positions, (0, 2, 1))
    hi = lax.reduce_precision(pos_t, exponent_bits=8, mantissa_bits=7)
    rest = pos_t - hi
    mid = lax.reduce_precision(rest, exponent_bits=8, mantissa_bits=7)
    pos_hi = hi.astype(jnp.bfloat16)
    pos_mid = mid.astype(jnp.bfloat16)
    pos_lo = (rest - mid).astype(jnp.bfloat16)
    spin_b = jnp.broadcast_to(spin_labels.astype(jnp.bfloat16)[None, :, None], (walkers_dev, elec_dev, 1))
    packed = jnp.concatenate([tokens, cotangent, pos_hi, pos_mid, pos_lo, spin_b], axis=-1)
    whole = lax.all_to_all(packed, "elec", 0, 0, tiled=True).reshape(elec_total, -1)
    walker_tok = whole[:, :features]
    walker_cot = whole[:, features : 2 * features]
    tail = whole[:, 2 * features :].astype(jnp.float32)
    walker_pos = (tail[:, 0:3] + tail[:, 3:6]) + tail[:, 6:9]
    spins = tail[:, 9]

    per_walker = walkers_dev // elec_size
    system = system_ids[lax.axis_index("elec") * per_walker]
    head_mat = lax.dynamic_index_in_dim(head_weight, system, 0, keepdims=False)

    msg_grads = jnp.dot(walker_cot, head_mat.T, preferred_element_type=jnp.float32).astype(jnp.bfloat16)
    tok_f = walker_tok.astype(jnp.float32)
    grads_f = msg_grads.astype(jnp.float32)

    spacing = cutoff_radius / (basis_count - 1)
    centers = jnp.arange(basis_count, dtype=jnp.float32) * spacing
    all_index = jnp.arange(elec_total, dtype=jnp.int32)
    block_rows = math.gcd(elec_total, 64)
    scaled_grads = msg_scale * grads_f

    block_count = elec_total // block_rows

    def block_terms(first):
        near_pos = lax.dynamic_slice_in_dim(walker_pos, first, block_rows, 0)
        near_spin = lax.dynamic_slice_in_dim(spins, first, block_rows, 0)
        near_index = first + jnp.arange(block_rows, dtype=jnp.int32)
        offsets = near_pos[:, None, :] - walker_pos[None, :, :]
        squares = offsets * offsets
        distance = jnp.sqrt(squares[..., 0] + squares[..., 1] + squares[..., 2])
        radial = jnp.exp(-jnp.square((distance[..., None] - centers) / spacing))
        same_spin = (near_spin[:, None] == spins[None, :])[..., None]
        nothing = jnp.zeros_like(radial)
        pair_feats = jnp.concatenate(
            [jnp.where(same_spin, radial, nothing), jnp.where(same_spin, nothing, radial)], axis=-1
        ).astype(jnp.bfloat16)
        pre_act = jnp.einsum("ijk,kf->ijf", pair_feats, filter_pairs, preferred_element_type=jnp.float32)
        off_diag = (near_index[:, None] != all_index[None, :])[..., None]
        return pair_feats, pre_act, logistic(pre_act), off_diag

    def weight_block(block_index, weight_run):
        first = block_index * block_rows
        pair_feats, pre_act, gate, off_diag = block_terms(first)
        near_grads = lax.dynamic_slice_in_dim(scaled_grads, first, block_rows, 0)
        slope = gate * (1.0 + pre_act * (1.0 - gate))
        pre_grad = near_grads[:, None, :] * tok_f[None, :, :] * slope
        pre_grad = jnp.where(off_diag, pre_grad, 0.0).astype(jnp.bfloat16)
        return weight_run + jnp.einsum("ijk,ijf->kf", pair_feats, pre_grad, preferred_element_type=jnp.float32)

    def message_block(first, tok_all, grads_all):
        unused_feats, pre_act, gate, off_diag = block_terms(first)
        filters = jnp.where(off_diag, pre_act * gate, 0.0).astype(jnp.bfloat16).astype(jnp.float32)
        return (jnp.sum(filters * tok_all[None, :, :], axis=1), jnp.sum(filters * grads_all[None, :, :], axis=1))

    weight_zero = jnp.zeros((2 * basis_count, features), jnp.float32)
    weight_sum = lax.fori_loop(0, block_count, weight_block, weight_zero)

    values = weight_sum
    msg_parts, back_parts = [], []
    walk_size, elec_size_ = lax.axis_size("walk"), lax.axis_size("elec")
    order = [("walk", 1), ("walk", 2)]
    order += [("elec", 1 << b) for b in range(max(elec_size_.bit_length() - 2, 0))]
    order += [("elec", elec_size_ // 2)]
    order += [("walk", 1 << b) for b in reversed(range(2, walk_size.bit_length() - 1))]
    for done, (axis, step) in enumerate(order):
        size = lax.axis_size(axis)
        pairs = [(i, i ^ step) for i in range(size)]
        if done < block_count:
            values, tok_b, grads_b = lax.optimization_barrier((values, tok_f, grads_f))
            arrived = lax.ppermute(values, axis, pairs)
            msg_rows, back_rows = message_block(done * block_rows, tok_b, grads_b)
            arrived, msg_rows, back_rows = lax.optimization_barrier((arrived, msg_rows, back_rows))
            msg_parts.append(msg_rows)
            back_parts.append(back_rows)
        else:
            arrived = lax.ppermute(values, axis, pairs)
        values = values + arrived
    weight_total = values
    msg_sum = jnp.concatenate(msg_parts, axis=0)
    back_sum = jnp.concatenate(back_parts, axis=0)

    messages = (msg_scale * msg_sum).astype(jnp.bfloat16)
    head_out = jnp.dot(messages, head_mat, preferred_element_type=jnp.float32)
    layer_out = (tok_f + head_out).astype(jnp.bfloat16)
    token_grad = walker_cot.astype(jnp.float32) + msg_scale * back_sum

    filter_grad = (grad_scale * weight_total).reshape(2, basis_count, features)

    result = jnp.concatenate([layer_out.astype(jnp.float32), token_grad], axis=-1)
    result = lax.all_to_all(result.reshape(elec_size, elec_dev, -1), "elec", 0, 0, tiled=True)
    return (result[..., :features].astype(jnp.bfloat16), result[..., features:], filter_grad)


def solution(mesh):
    in_specs = (
        P("walk", "elec", None),
        P("walk", None, "elec"),
        P("elec"),
        P("walk"),
        P(),
        P(),
        P("walk", "elec", None),
    )
    out_specs = (P("walk", "elec", None), P("walk", "elec", None), P())
    return jax.shard_map(body, mesh=mesh, in_specs=in_specs, out_specs=out_specs, check_vma=False)
```

```python
import math

import jax
import jax.numpy as jnp
from jax import lax
from jax.sharding import PartitionSpec as P

cutoff_radius = 8.0


def logistic(values):
    return 0.5 * jnp.tanh(0.5 * values) + 0.5


def butterfly_sum(values, axes):
    for axis in axes:
        size = lax.axis_size(axis)
        step = 1
        while step < size:
            pairs = [(i, i ^ step) for i in range(size)]
            values = values + lax.ppermute(values, axis, pairs)
            step *= 2
    return values


def body(tokens, positions, spin_labels, system_ids, filter_weight, head_weight, cotangent):
    walkers_dev, elec_dev, features = tokens.shape
    basis_count = filter_weight.shape[1]
    elec_size = lax.axis_size("elec")
    elec_total = elec_dev * elec_size
    walker_total = walkers_dev * lax.axis_size("walk")
    msg_scale = 1.0 / math.sqrt(elec_total)
    grad_scale = 1.0 / math.sqrt(walker_total * elec_total)
    filter_pairs = filter_weight.reshape(2 * basis_count, features)

    pos_t = jnp.transpose(positions, (0, 2, 1))
    hi = lax.reduce_precision(pos_t, exponent_bits=8, mantissa_bits=7)
    rest = pos_t - hi
    mid = lax.reduce_precision(rest, exponent_bits=8, mantissa_bits=7)
    pos_hi = hi.astype(jnp.bfloat16)
    pos_mid = mid.astype(jnp.bfloat16)
    pos_lo = (rest - mid).astype(jnp.bfloat16)
    spin_b = jnp.broadcast_to(spin_labels.astype(jnp.bfloat16)[None, :, None], (walkers_dev, elec_dev, 1))
    packed = jnp.concatenate([tokens, cotangent, pos_hi, pos_mid, pos_lo, spin_b], axis=-1)
    whole = lax.all_to_all(packed, "elec", 0, 0, tiled=True).reshape(elec_total, -1)
    walker_tok = whole[:, :features]
    walker_cot = whole[:, features : 2 * features]
    tail = whole[:, 2 * features :].astype(jnp.float32)
    walker_pos = (tail[:, 0:3] + tail[:, 3:6]) + tail[:, 6:9]
    spins = tail[:, 9]

    per_walker = walkers_dev // elec_size
    system = system_ids[lax.axis_index("elec") * per_walker]
    head_mat = lax.dynamic_index_in_dim(head_weight, system, 0, keepdims=False)

    msg_grads = jnp.dot(walker_cot, head_mat.T, preferred_element_type=jnp.float32).astype(jnp.bfloat16)
    tok_f = walker_tok.astype(jnp.float32)
    grads_f = msg_grads.astype(jnp.float32)

    spacing = cutoff_radius / (basis_count - 1)
    centers = jnp.arange(basis_count, dtype=jnp.float32) * spacing
    all_index = jnp.arange(elec_total, dtype=jnp.int32)
    block_rows = math.gcd(elec_total, 64)
    scaled_grads = msg_scale * grads_f

    block_count = elec_total // block_rows

    def block_terms(first):
        near_pos = lax.dynamic_slice_in_dim(walker_pos, first, block_rows, 0)
        near_spin = lax.dynamic_slice_in_dim(spins, first, block_rows, 0)
        near_index = first + jnp.arange(block_rows, dtype=jnp.int32)
        offsets = near_pos[:, None, :] - walker_pos[None, :, :]
        squares = offsets * offsets
        distance = jnp.sqrt(squares[..., 0] + squares[..., 1] + squares[..., 2])
        radial = jnp.exp(-jnp.square((distance[..., None] - centers) / spacing))
        same_spin = (near_spin[:, None] == spins[None, :])[..., None]
        nothing = jnp.zeros_like(radial)
        pair_feats = jnp.concatenate(
            [jnp.where(same_spin, radial, nothing), jnp.where(same_spin, nothing, radial)], axis=-1
        ).astype(jnp.bfloat16)
        pre_act = jnp.einsum("ijk,kf->ijf", pair_feats, filter_pairs, preferred_element_type=jnp.float32)
        off_diag = (near_index[:, None] != all_index[None, :])[..., None]
        return pair_feats, pre_act, logistic(pre_act), off_diag

    def weight_block(block_index, weight_run):
        first = block_index * block_rows
        pair_feats, pre_act, gate, off_diag = block_terms(first)
        near_grads = lax.dynamic_slice_in_dim(scaled_grads, first, block_rows, 0)
        slope = gate * (1.0 + pre_act * (1.0 - gate))
        pre_grad = near_grads[:, None, :] * tok_f[None, :, :] * slope
        pre_grad = jnp.where(off_diag, pre_grad, 0.0).astype(jnp.bfloat16)
        return weight_run + jnp.einsum("ijk,ijf->kf", pair_feats, pre_grad, preferred_element_type=jnp.float32)

    def message_block(first, tok_all, grads_all):
        unused_feats, pre_act, gate, off_diag = block_terms(first)
        filters = jnp.where(off_diag, pre_act * gate, 0.0).astype(jnp.bfloat16).astype(jnp.float32)
        return (jnp.sum(filters * tok_all[None, :, :], axis=1), jnp.sum(filters * grads_all[None, :, :], axis=1))

    weight_zero = jnp.zeros((2 * basis_count, features), jnp.float32)
    weight_sum = lax.fori_loop(0, block_count, weight_block, weight_zero)

    values = weight_sum
    msg_parts, back_parts = [], []
    walk_size, elec_size_ = lax.axis_size("walk"), lax.axis_size("elec")
    order = [("walk", 1), ("walk", 2)]
    order += [("elec", 1 << b) for b in range(max(elec_size_.bit_length() - 2, 0))]
    z_steps = [("walk", 1 << b) for b in range(2, walk_size.bit_length() - 1)]
    order += z_steps[:1] + [("elec", elec_size_ // 2)] + z_steps[1:]
    for done, (axis, step) in enumerate(order):
        size = lax.axis_size(axis)
        pairs = [(i, i ^ step) for i in range(size)]
        if done < block_count:
            values, tok_b, grads_b = lax.optimization_barrier((values, tok_f, grads_f))
            arrived = lax.ppermute(values, axis, pairs)
            msg_rows, back_rows = message_block(done * block_rows, tok_b, grads_b)
            arrived, msg_rows, back_rows = lax.optimization_barrier((arrived, msg_rows, back_rows))
            msg_parts.append(msg_rows)
            back_parts.append(back_rows)
        else:
            arrived = lax.ppermute(values, axis, pairs)
        values = values + arrived
    weight_total = values
    msg_sum = jnp.concatenate(msg_parts, axis=0)
    back_sum = jnp.concatenate(back_parts, axis=0)

    messages = (msg_scale * msg_sum).astype(jnp.bfloat16)
    head_out = jnp.dot(messages, head_mat, preferred_element_type=jnp.float32)
    layer_out = (tok_f + head_out).astype(jnp.bfloat16)
    token_grad = walker_cot.astype(jnp.float32) + msg_scale * back_sum

    filter_grad = (grad_scale * weight_total).reshape(2, basis_count, features)

    result = jnp.concatenate([layer_out.astype(jnp.float32), token_grad], axis=-1)
    result = lax.all_to_all(result.reshape(elec_size, elec_dev, -1), "elec", 0, 0, tiled=True)
    return (result[..., :features].astype(jnp.bfloat16), result[..., features:], filter_grad)


def solution(mesh):
    in_specs = (
        P("walk", "elec", None),
        P("walk", None, "elec"),
        P("elec"),
        P("walk"),
        P(),
        P(),
        P("walk", "elec", None),
    )
    out_specs = (P("walk", "elec", None), P("walk", "elec", None), P())
    return jax.shard_map(body, mesh=mesh, in_specs=in_specs, out_specs=out_specs, check_vma=False)
```

```python
import math

import jax
import jax.numpy as jnp
from jax import lax
from jax.sharding import PartitionSpec as P

cutoff_radius = 8.0


def logistic(values):
    return 0.5 * jnp.tanh(0.5 * values) + 0.5


def butterfly_sum(values, axes):
    for axis in axes:
        size = lax.axis_size(axis)
        step = 1
        while step < size:
            pairs = [(i, i ^ step) for i in range(size)]
            values = values + lax.ppermute(values, axis, pairs)
            step *= 2
    return values


def body(tokens, positions, spin_labels, system_ids, filter_weight, head_weight, cotangent):
    walkers_dev, elec_dev, features = tokens.shape
    basis_count = filter_weight.shape[1]
    elec_size = lax.axis_size("elec")
    elec_total = elec_dev * elec_size
    walker_total = walkers_dev * lax.axis_size("walk")
    msg_scale = 1.0 / math.sqrt(elec_total)
    grad_scale = 1.0 / math.sqrt(walker_total * elec_total)
    filter_pairs = filter_weight.reshape(2 * basis_count, features)

    pos_t = jnp.transpose(positions, (0, 2, 1))
    hi = lax.reduce_precision(pos_t, exponent_bits=8, mantissa_bits=7)
    rest = pos_t - hi
    mid = lax.reduce_precision(rest, exponent_bits=8, mantissa_bits=7)
    pos_hi = hi.astype(jnp.bfloat16)
    pos_mid = mid.astype(jnp.bfloat16)
    pos_lo = (rest - mid).astype(jnp.bfloat16)
    spin_b = jnp.broadcast_to(spin_labels.astype(jnp.bfloat16)[None, :, None], (walkers_dev, elec_dev, 1))
    packed = jnp.concatenate([tokens, cotangent, pos_hi, pos_mid, pos_lo, spin_b], axis=-1)
    whole = lax.all_to_all(packed, "elec", 0, 0, tiled=True).reshape(elec_total, -1)
    walker_tok = whole[:, :features]
    walker_cot = whole[:, features : 2 * features]
    tail = whole[:, 2 * features :].astype(jnp.float32)
    walker_pos = (tail[:, 0:3] + tail[:, 3:6]) + tail[:, 6:9]
    spins = tail[:, 9]

    per_walker = walkers_dev // elec_size
    system = system_ids[lax.axis_index("elec") * per_walker]
    head_mat = lax.dynamic_index_in_dim(head_weight, system, 0, keepdims=False)

    msg_grads = jnp.dot(walker_cot, head_mat.T, preferred_element_type=jnp.float32).astype(jnp.bfloat16)
    tok_f = walker_tok.astype(jnp.float32)
    grads_f = msg_grads.astype(jnp.float32)

    spacing = cutoff_radius / (basis_count - 1)
    centers = jnp.arange(basis_count, dtype=jnp.float32) * spacing
    all_index = jnp.arange(elec_total, dtype=jnp.int32)
    block_rows = math.gcd(elec_total, 64)
    scaled_grads = msg_scale * grads_f

    block_count = elec_total // block_rows

    def block_terms(first):
        near_pos = lax.dynamic_slice_in_dim(walker_pos, first, block_rows, 0)
        near_spin = lax.dynamic_slice_in_dim(spins, first, block_rows, 0)
        near_index = first + jnp.arange(block_rows, dtype=jnp.int32)
        offsets = near_pos[:, None, :] - walker_pos[None, :, :]
        squares = offsets * offsets
        distance = jnp.sqrt(squares[..., 0] + squares[..., 1] + squares[..., 2])
        radial = jnp.exp(-jnp.square((distance[..., None] - centers) / spacing))
        same_spin = (near_spin[:, None] == spins[None, :])[..., None]
        nothing = jnp.zeros_like(radial)
        pair_feats = jnp.concatenate(
            [jnp.where(same_spin, radial, nothing), jnp.where(same_spin, nothing, radial)], axis=-1
        ).astype(jnp.bfloat16)
        pre_act = jnp.einsum("ijk,kf->ijf", pair_feats, filter_pairs, preferred_element_type=jnp.float32)
        off_diag = (near_index[:, None] != all_index[None, :])[..., None]
        return pair_feats, pre_act, logistic(pre_act), off_diag

    def weight_block(block_index, weight_run):
        first = block_index * block_rows
        pair_feats, pre_act, gate, off_diag = block_terms(first)
        near_grads = lax.dynamic_slice_in_dim(scaled_grads, first, block_rows, 0)
        slope = gate * (1.0 + pre_act * (1.0 - gate))
        pre_grad = near_grads[:, None, :] * tok_f[None, :, :] * slope
        pre_grad = jnp.where(off_diag, pre_grad, 0.0).astype(jnp.bfloat16)
        return weight_run + jnp.einsum("ijk,ijf->kf", pair_feats, pre_grad, preferred_element_type=jnp.float32)

    def message_block(first, tok_all, grads_all):
        unused_feats, pre_act, gate, off_diag = block_terms(first)
        filters = jnp.where(off_diag, pre_act * gate, 0.0).astype(jnp.bfloat16).astype(jnp.float32)
        return (jnp.sum(filters * tok_all[None, :, :], axis=1), jnp.sum(filters * grads_all[None, :, :], axis=1))

    weight_zero = jnp.zeros((2 * basis_count, features), jnp.float32)
    weight_sum = lax.fori_loop(0, block_count, weight_block, weight_zero)

    values = weight_sum
    msg_parts, back_parts = [], []
    walk_size, elec_size_ = lax.axis_size("walk"), lax.axis_size("elec")
    order = [("elec", 1), ("walk", 1), ("walk", 2)]
    order += [("elec", 1 << b) for b in range(1, max(elec_size_.bit_length() - 2, 0))]
    order += [("elec", elec_size_ // 2)]
    order += [("walk", 1 << b) for b in range(2, walk_size.bit_length() - 1)]
    for done, (axis, step) in enumerate(order):
        size = lax.axis_size(axis)
        pairs = [(i, i ^ step) for i in range(size)]
        if done < block_count:
            values, tok_b, grads_b = lax.optimization_barrier((values, tok_f, grads_f))
            arrived = lax.ppermute(values, axis, pairs)
            msg_rows, back_rows = message_block(done * block_rows, tok_b, grads_b)
            arrived, msg_rows, back_rows = lax.optimization_barrier((arrived, msg_rows, back_rows))
            msg_parts.append(msg_rows)
            back_parts.append(back_rows)
        else:
            arrived = lax.ppermute(values, axis, pairs)
        values = values + arrived
    weight_total = values
    msg_sum = jnp.concatenate(msg_parts, axis=0)
    back_sum = jnp.concatenate(back_parts, axis=0)

    messages = (msg_scale * msg_sum).astype(jnp.bfloat16)
    head_out = jnp.dot(messages, head_mat, preferred_element_type=jnp.float32)
    layer_out = (tok_f + head_out).astype(jnp.bfloat16)
    token_grad = walker_cot.astype(jnp.float32) + msg_scale * back_sum

    filter_grad = (grad_scale * weight_total).reshape(2, basis_count, features)

    result = jnp.concatenate([layer_out.astype(jnp.float32), token_grad], axis=-1)
    result = lax.all_to_all(result.reshape(elec_size, elec_dev, -1), "elec", 0, 0, tiled=True)
    return (result[..., :features].astype(jnp.bfloat16), result[..., features:], filter_grad)


def solution(mesh):
    in_specs = (
        P("walk", "elec", None),
        P("walk", None, "elec"),
        P("elec"),
        P("walk"),
        P(),
        P(),
        P("walk", "elec", None),
    )
    out_specs = (P("walk", "elec", None), P("walk", "elec", None), P())
    return jax.shard_map(body, mesh=mesh, in_specs=in_specs, out_specs=out_specs, check_vma=False)
```
